512 devices in a mesh: mesh: 128 (over y, z, core), sect: 4 (over x).
Axes of the slice: x: 4, y: 8, z: 8, core: 2. Of those that a mesh axis runs over, the one named last changes fastest.
Arguments:
- fields: float32 [5, 125, 131072], P(None, None, ('mesh', 'sect')), may hold values from -6 to 6
- segment_register: float32 [5, 125, 131072], P(None, None, ('mesh', 'sect')), may hold values from -6 to 6
- volume_operator: float32 [3, 125, 125], replicated, may hold values from -0.5 to 0.5
- flux_jacobian: float32 [3, 5, 5], replicated, may hold values from -2.5 to 2.5
- penalty: float32 [5], replicated, may hold values from 0.5 to 2
- face_element: int32 [2048], P(('mesh', 'sect')), may hold values from 0 to 255
- rotation: int32 [4], P('sect'), may hold values from 0 to 511
- pressure_history: bfloat16 [15, 2048], P(None, ('mesh', 'sect')), may hold values from -6 to 6
- surface_geometry: bfloat16 [6, 2048], P(None, ('mesh', 'sect')), may hold values from -1 to 1
- observer_sites: float32 [3, 65536], P(None, ('mesh', 'sect')), may hold values from -6 to 6, as said below
- delay_table: int32 [512, 512], P(None, ('mesh', 'sect')), may hold values from 0 to 7
Outputs:
- new_fields: float32 [5, 125, 131072], P(None, None, ('mesh', 'sect'))
- new_register: float32 [5, 125, 131072], P(None, None, ('mesh', 'sect'))
- far_pressure: float32 [8, 65536], P(None, ('mesh', 'sect'))
The draws below stay inside these ranges and needn't reach their ends.
Inputs may be any that keep to these rules, and one draw needn't show every extreme that they name: `observer_sites`: every coordinate has magnitude 2 to 6.
All inputs are finite; a program needn't handle non-finite values.
Results may differ from the reference program's by a relative error of at most 0.0039.
Values may be sent and summed in bfloat16 or wider, within the bound.
No kernel may reach another device: no remote copies, remote signals or barrier semaphores. Data moves between devices by JAX's collectives and lax.ppermute only.
A program may use at most 64 MiB of HBM per device.

```python
import math
import jax
import jax.numpy as jnp
from jax import lax

VARS = 5
NODES = 125
ELEM_DEV = 256
FACE_DEV = 4
OBS_DEV = 128
TB = 8
NB = 8
HIST = 16
CYCLE = 512
ELEMS = 131072
SURF = 2048
OBS = 65536
N_MESH = 128
N_SECT = 4
DEVICES = 512


def draw_observer_sites(key, part):
    sign_key, size_key = jax.random.split(key)
    signs = jax.random.randint(sign_key, (3, OBS), 0, 2).astype(jnp.float32) * 2.0 - 1.0
    spread = jax.random.uniform(size_key, (3, OBS), jnp.float32)
    magnitude = 2.0 + 4.0 * spread
    return signs * magnitude


def draw_rotation(key, part):
    base_key, within_key, order_key = jax.random.split(jax.random.fold_in(key, 71), 3)
    base = jax.random.randint(base_key, (N_SECT,), 0, CYCLE)
    within = jax.random.randint(within_key, (N_SECT,), 1, FACE_DEV)
    order = jax.random.permutation(order_key, N_SECT)
    halfway = CYCLE // 2 + within
    last_value = jnp.zeros_like(base) + (CYCLE - 1)
    chosen = jnp.where(order == 0, halfway, jnp.where(order == 1, last_value, base))
    return chosen.astype(jnp.int32)


def place_ends(values, rng, low, high):
    place = [jax.random.randint(jax.random.fold_in(rng, axis), (), 0, length) for axis, length in enumerate(values.shape)]
    widest = values.shape.index(max(values.shape))
    beside = place[:widest] + [(place[widest] + 1) % values.shape[widest]] + place[widest + 1:]
    return values.at[tuple(place)].set(low).at[tuple(beside)].set(high)


def shard_levels(own_key, shape, cuts, least, high):
    factor_of, own = 1.0, jax.random.fold_in(own_key, 6)
    for axis_at, shards_of in cuts:
        steps = jnp.exp(jax.random.uniform(jax.random.fold_in(own, axis_at), (shards_of,), jnp.float32, least / len(cuts), high / len(cuts)))
        factor_of = factor_of * jnp.repeat(steps, shape[axis_at] // shards_of).reshape([-1 if axis == axis_at else 1 for axis in range(len(shape))])
    return factor_of


def noise(key, shape, width, most, cuts=(), held_as=jnp.bfloat16):
    result = jax.random.normal(key, shape, jnp.float32) * width
    if len(cuts) > 0:
        result = shard_levels(key, shape, cuts, -0.22, 0.18) * result
    return jnp.clip(result, min=-most, max=most).astype(held_as)


def setup_inputs(seed: int = 0) -> dict:
    keys = jax.random.split(jax.random.key(seed), 12)
    fields = noise(keys[0], (VARS, NODES, ELEMS), 1.0, 6.0, ((2, 512),), jnp.float32)
    segment_register = noise(keys[1], (VARS, NODES, ELEMS), 1.0, 6.0, ((2, 512),), jnp.float32)
    volume_operator = noise(keys[2], (3, NODES, NODES), NODES ** -0.5, 0.5, (), jnp.float32)
    flux_jacobian = noise(keys[3], (3, VARS, VARS), VARS ** -0.5, 2.5, (), jnp.float32)
    penalty = jnp.clip(jnp.exp(jax.random.uniform(keys[4], (VARS,), jnp.float32, math.log(0.5), math.log(2.0))), 0.5, 2.0)
    face_element = place_ends(jax.random.randint(keys[5], (SURF,), 0, ELEM_DEV), jax.random.fold_in(keys[5], 1), 0, ELEM_DEV - 1).astype(jnp.int32)
    rotation = draw_rotation(jax.random.fold_in(keys[11], 71), 0)
    pressure_history = noise(keys[7], (HIST - 1, SURF), 1.0, 6.0, ((1, 512),))
    surface_geometry = jnp.clip(jax.random.uniform(keys[8], (6, SURF), jnp.float32, -1.0, 1.0) * shard_levels(keys[8], (6, SURF), ((1, 512),), -0.4, 0.0), -1.0, 1.0).astype(jnp.bfloat16)
    observer_sites = draw_observer_sites(jax.random.fold_in(keys[11], 71), 0)
    delay_table = place_ends(jax.random.randint(keys[10], (DEVICES, DEVICES), 0, NB), jax.random.fold_in(keys[10], 1), 0, NB - 1).astype(jnp.int32)
    return {"fields": fields, "segment_register": segment_register, "volume_operator": volume_operator, "flux_jacobian": flux_jacobian, "penalty": penalty, "face_element": face_element, "rotation": rotation, "pressure_history": pressure_history, "surface_geometry": surface_geometry, "observer_sites": observer_sites, "delay_table": delay_table}


segment_decay = -0.4178904745
segment_gain = 1.4061
time_step = 0.2
four_pi = 12.566370614359172
highest_value = lax.Precision.HIGHEST

def cycle_roll(values, shift_by):
    lead = values.shape[:-3]
    moved_axes = jnp.swapaxes(values, -3, -2)
    flat = moved_axes.reshape(lead + (N_SECT, N_MESH * ELEM_DEV))
    flat = jnp.roll(flat, shift_by, axis=-1)
    return jnp.swapaxes(flat.reshape(lead + (N_SECT, N_MESH, ELEM_DEV)), -3, -2)

def section_shift(values, upward):
    zeros_edge = jnp.zeros_like(values[..., :1, :])
    if upward:
        return jnp.concatenate([zeros_edge, values[..., :-1, :]], axis=-2)
    return jnp.concatenate([values[..., 1:, :], zeros_edge], axis=-2)

def far_kernels(geometry, observers):
    separation = observers[:, None, :] - geometry[:3, :, None]
    square = lax.optimization_barrier(jnp.sum(separation * separation, axis=0))
    radius = jnp.sqrt(square)
    normal_part = lax.optimization_barrier(jnp.sum(geometry[3:6, :, None] * separation, axis=0))
    near_kernel = (normal_part / (four_pi * square * radius)).astype(jnp.bfloat16)
    rate_kernel = (normal_part / (four_pi * square)).astype(jnp.bfloat16)
    return (near_kernel, rate_kernel)

def reference(fields, segment_register, volume_operator, flux_jacobian, penalty, face_element, rotation, pressure_history, surface_geometry, observer_sites, delay_table):
    rate_tendency = jnp.zeros(fields.shape, jnp.float32)
    for spatial_direction in range(3):
        derived_quantity = jnp.einsum('nm,wme->wne', volume_operator[spatial_direction], fields, precision=highest_value)
        rate_tendency = rate_tendency + jnp.einsum('so,oyx->syx', flux_jacobian[spatial_direction], derived_quantity, precision=highest_value)
    nodal_grid = fields.reshape(VARS, 5, 5, 5, N_MESH, N_SECT, ELEM_DEV)
    weight = penalty.reshape(VARS, 1, 1, 1, 1, 1)
    west_face = nodal_grid[:, :, 0]
    east_face = nodal_grid[:, :, 4]
    west_beyond = cycle_roll(east_face, 1)
    east_beyond = cycle_roll(west_face, -1)
    lower_face = nodal_grid[:, :, :, 0]
    upper_face = nodal_grid[:, :, :, 4]
    lower_beyond = section_shift(upper_face, True)
    upper_beyond = section_shift(lower_face, False)
    inner_face = nodal_grid[:, 0].reshape(VARS, 25, N_MESH, N_SECT, ELEM_DEV)
    outer_face = nodal_grid[:, 4].reshape(VARS, 25, N_MESH, N_SECT, ELEM_DEV)
    element_map = face_element.reshape(N_MESH, N_SECT, FACE_DEV)
    selector = (element_map[..., None] == jnp.arange(ELEM_DEV).astype(jnp.int32)).astype(jnp.float32)
    rotor_rows = jnp.einsum('vqmke,mkfe->vqmkf', inner_face, selector, precision=highest_value)
    stator = jnp.einsum('vqmke,mkfe->vqmkf', outer_face, selector, precision=highest_value)
    cycle_rows = jnp.transpose(rotor_rows, (0, 1, 3, 2, 4)).reshape(VARS, 25, N_SECT, CYCLE)
    cycle_position = (jnp.arange(CYCLE).astype(jnp.int32)[None, :] + rotation[:, None]) % CYCLE
    rotated_cycle = jnp.take_along_axis(cycle_rows, jnp.broadcast_to(cycle_position[None, None], cycle_rows.shape), axis=3)
    rotated = jnp.transpose(rotated_cycle.reshape(VARS, 25, N_SECT, N_MESH, FACE_DEV), (0, 1, 3, 2, 4))
    mortar = penalty.reshape(VARS, 1, 1, 1, 1) * (rotated - stator)
    mortar_lift = jnp.einsum('vqmkf,mkfe->vqmke', mortar, selector, precision=highest_value).reshape(VARS, 5, 5, N_MESH, N_SECT, ELEM_DEV)
    tendency_grid = rate_tendency.reshape(VARS, 5, 5, 5, N_MESH, N_SECT, ELEM_DEV)
    tendency_grid = tendency_grid.at[:, :, 0].add(weight * (west_beyond - west_face))
    tendency_grid = tendency_grid.at[:, :, 4].add(weight * (east_beyond - east_face))
    tendency_grid = tendency_grid.at[:, :, :, 0].add(weight * (lower_beyond - lower_face))
    tendency_grid = tendency_grid.at[:, :, :, 4].add(weight * (upper_beyond - upper_face))
    tendency_grid = tendency_grid.at[:, 4].add(mortar_lift)
    rate_tendency = tendency_grid.reshape(VARS, NODES, ELEMS)
    new_register = segment_decay * segment_register + time_step * rate_tendency
    new_fields = fields + segment_gain * new_register
    top_layer = new_fields.reshape(VARS, 5, 5, 5, N_MESH, N_SECT, ELEM_DEV)[VARS - 1, 4].reshape(25, N_MESH, N_SECT, ELEM_DEV)
    sampled = jnp.einsum('qmke,mkfe->qmkf', top_layer, selector, precision=highest_value)
    surface_now = lax.optimization_barrier(jnp.mean(sampled, axis=0)).reshape(SURF)
    history = jnp.concatenate([pressure_history, surface_now[None].astype(jnp.bfloat16)], axis=0)
    geometry = surface_geometry.astype(jnp.float32)
    block_of = jnp.arange(SURF).astype(jnp.int32) // FACE_DEV

    def one_block(block):
        observers = lax.dynamic_slice_in_dim(observer_sites, block * OBS_DEV, OBS_DEV, 1)
        column_delays = lax.dynamic_index_in_dim(delay_table, block, 1, keepdims=False)
        delays = column_delays[block_of]
        row_index = (NB - 1 - delays)[None, :] + jnp.arange(TB + 1).astype(jnp.int32)[:, None]
        window = jnp.take_along_axis(history, row_index, axis=0)
        window_late = window[1:]
        change = (window_late.astype(jnp.float32) - window[:-1].astype(jnp.float32)).astype(jnp.bfloat16)
        near_kernel, rate_kernel = far_kernels(geometry, observers)
        return jnp.dot(window_late, near_kernel, preferred_element_type=jnp.float32) + jnp.dot(change, rate_kernel, preferred_element_type=jnp.float32)
    distant_blocks = lax.map(one_block, jnp.arange(DEVICES).astype(jnp.int32))
    far_pressure = jnp.transpose(distant_blocks, (1, 0, 2)).reshape(TB, OBS)
    return (new_fields, new_register, far_pressure)
```

```python
import numpy as np
import jax
import jax.numpy as jnp
from jax import lax
from jax.sharding import PartitionSpec as P

VARS = 5
NODES = 125
FACE_DEV = 4
TB = 8
NB = 8

segment_decay = -0.4178904745
segment_gain = 1.4061
time_step = 0.2
four_pi = 12.566370614359172
highest_value = lax.Precision.HIGHEST
ALL = ("mesh", "sect")


def node_tables():
    a, b, c = np.meshgrid(np.arange(5), np.arange(5), np.arange(5), indexing="ij")
    a, b, c = a.reshape(-1), b.reshape(-1), c.reshape(-1)
    n = np.arange(NODES)
    west = np.zeros((NODES, NODES), np.float32)
    west[n[b == 0], n[b == 0] + 20] = 1.0
    east = np.zeros((NODES, NODES), np.float32)
    east[n[b == 4], n[b == 4] - 20] = 1.0
    take_c4 = np.zeros((25, NODES), np.float32)
    take_c4[np.arange(25), n[c == 4]] = 1.0
    take_c0 = np.zeros((25, NODES), np.float32)
    take_c0[np.arange(25), n[c == 0]] = 1.0
    count = ((b == 0).astype(np.float32) + (b == 4) + (c == 0) + (c == 4)).reshape(1, NODES, 1)
    return west, east, take_c4, take_c0, count


def flat_gather(value, axes):
    size = value.size
    whole = lax.all_gather(value.reshape(size), axes, axis=0, tiled=True)
    return whole.reshape((-1,) + value.shape)


def far_kernels(geometry, observers):
    separation = observers[:, None, :] - geometry[:3, :, None]
    square = jnp.sum(separation * separation, axis=0)
    radius = jnp.sqrt(square)
    normal_part = jnp.sum(geometry[3:6, :, None] * separation, axis=0)
    near_kernel = (normal_part / (four_pi * square * radius)).astype(jnp.bfloat16)
    rate_kernel = (normal_part / (four_pi * square)).astype(jnp.bfloat16)
    return (near_kernel, rate_kernel)


def per_device(
    fields,
    segment_register,
    volume_operator,
    flux_jacobian,
    penalty,
    face_element,
    rotation,
    pressure_history,
    surface_geometry,
    observer_sites,
    delay_table,
):
    elements = fields.shape[2]
    face_count = face_element.shape[0]
    west_np, east_np, take_c4_np, take_c0_np, count_np = node_tables()
    west_sel = jnp.asarray(west_np)
    east_sel = jnp.asarray(east_np)
    take_c4 = jnp.asarray(take_c4_np)
    take_c0 = jnp.asarray(take_c0_np)
    weight = penalty.reshape(VARS, 1, 1)

    early = jnp.concatenate([pressure_history, surface_geometry], axis=0)
    early_all = flat_gather(early, ALL)
    early_all = jnp.transpose(early_all, (1, 0, 2)).reshape(early.shape[0], -1)
    old_history = early_all[: pressure_history.shape[0]]
    geometry = early_all[pressure_history.shape[0] :].astype(jnp.float32)

    selector = (face_element[:, None] == jnp.arange(elements, dtype=jnp.int32)[None, :]).astype(
        jnp.float32
    )
    rotor_rows = jnp.einsum("vqe,fe->vqf", fields[:, 0:25], selector, precision=highest_value)
    whole_cycle = flat_gather(rotor_rows, "mesh")
    cycle_size = face_count * lax.axis_size("mesh")
    whole_cycle = jnp.transpose(whole_cycle, (1, 2, 0, 3)).reshape(VARS, 25, cycle_size)

    west_part = jnp.einsum("nm,vme->vne", west_sel, fields, precision=highest_value)
    east_part = jnp.einsum("nm,vme->vne", east_sel, fields, precision=highest_value)
    mesh_size = lax.axis_size("mesh")
    forward = [(i, (i + 1) % mesh_size) for i in range(mesh_size)]
    backward = [(j, i) for i, j in forward]
    west_halo = lax.ppermute(west_part[:, :, elements - 1 :], "mesh", forward)
    east_halo = lax.ppermute(east_part[:, :, :1], "mesh", backward)
    sect_size = lax.axis_size("sect")
    upward = [(i, i + 1) for i in range(sect_size - 1)]
    downward = [(j, i) for i, j in upward]
    top_rows = jnp.einsum("jm,vme->vje", take_c4, fields, precision=highest_value)
    bottom_rows = jnp.einsum("jm,vme->vje", take_c0, fields, precision=highest_value)
    from_below = lax.ppermute(top_rows, "sect", upward)
    from_above = lax.ppermute(bottom_rows, "sect", downward)

    combined = jnp.einsum(
        "dso,dnm->snom", flux_jacobian, volume_operator, precision=highest_value
    )
    volume = jnp.einsum("snom,ome->sne", combined, fields, precision=highest_value)

    west_beyond = jnp.concatenate([west_halo, west_part[:, :, : elements - 1]], axis=2)
    east_beyond = jnp.concatenate([east_part[:, :, 1:], east_halo], axis=2)
    lower_beyond = jnp.einsum("jn,vje->vne", take_c0, from_below, precision=highest_value)
    upper_beyond = jnp.einsum("jn,vje->vne", take_c4, from_above, precision=highest_value)

    offset = rotation[0]
    doubled = jnp.concatenate([whole_cycle, whole_cycle], axis=2)
    slice_start = (lax.axis_index("mesh") * face_count + offset) % cycle_size
    rotated = lax.dynamic_slice_in_dim(doubled, slice_start, face_count, 2)
    stator = jnp.einsum("vqe,fe->vqf", fields[:, 100:125], selector, precision=highest_value)
    mortar = weight * (rotated - stator)
    mortar_lift = jnp.einsum("vqf,fe->vqe", mortar, selector, precision=highest_value)
    mortar_full = jnp.concatenate(
        [jnp.zeros((VARS, 100, elements), jnp.float32), mortar_lift], axis=1
    )

    neighbours = west_beyond + east_beyond + lower_beyond + upper_beyond
    rate_tendency = (
        volume + weight * (neighbours - jnp.asarray(count_np) * fields) + mortar_full
    )
    new_register = segment_decay * segment_register + time_step * rate_tendency
    new_fields = fields + segment_gain * new_register

    sampled = jnp.einsum(
        "qe,fe->qf", new_fields[VARS - 1, 100:125], selector, precision=highest_value
    )
    surface_now = jnp.mean(sampled, axis=0).astype(jnp.bfloat16)
    now_all = flat_gather(surface_now, ALL).reshape(1, -1)
    history = jnp.concatenate([old_history, now_all], axis=0)

    my_delays = delay_table[:, 0]
    delays = jnp.repeat(my_delays, FACE_DEV)
    window = jnp.zeros((TB + 1, history.shape[1]), history.dtype)
    for bin_ in range(NB):
        window = jnp.where(
            (delays == bin_)[None, :], history[NB - 1 - bin_ : NB - 1 - bin_ + TB + 1], window
        )
    window_late = window[1:]
    change = (window_late.astype(jnp.float32) - window[:-1].astype(jnp.float32)).astype(
        jnp.bfloat16
    )
    near_kernel, rate_kernel = far_kernels(geometry, observer_sites)
    running = jnp.dot(window_late, near_kernel, preferred_element_type=jnp.float32) + jnp.dot(
        change, rate_kernel, preferred_element_type=jnp.float32
    )
    return (new_fields, new_register, running)


def solution(mesh):
    placed = (
        P(None, None, ALL),
        P(None, None, ALL),
        P(),
        P(),
        P(),
        P(ALL),
        P("sect"),
        P(None, ALL),
        P(None, ALL),
        P(None, ALL),
        P(None, ALL),
    )
    return jax.shard_map(
        per_device,
        mesh=mesh,
        in_specs=placed,
        out_specs=(
            P(None, None, ALL),
            P(None, None, ALL),
            P(None, ALL),
        ),
        check_vma=False,
    )
```

```python
import numpy as np
import jax
import jax.numpy as jnp
from jax import lax
from jax.sharding import PartitionSpec as P

VARS = 5
NODES = 125
FACE_DEV = 4
TB = 8
NB = 8

segment_decay = -0.4178904745
segment_gain = 1.4061
time_step = 0.2
four_pi = 12.566370614359172
highest_value = lax.Precision.HIGHEST
ALL = ("mesh", "sect")


def node_tables():
    a, b, c = np.meshgrid(np.arange(5), np.arange(5), np.arange(5), indexing="ij")
    a, b, c = a.reshape(-1), b.reshape(-1), c.reshape(-1)
    n = np.arange(NODES)
    west = np.zeros((NODES, NODES), np.float32)
    west[n[b == 0], n[b == 0] + 20] = 1.0
    east = np.zeros((NODES, NODES), np.float32)
    east[n[b == 4], n[b == 4] - 20] = 1.0
    take_c4 = np.zeros((25, NODES), np.float32)
    take_c4[np.arange(25), n[c == 4]] = 1.0
    take_c0 = np.zeros((25, NODES), np.float32)
    take_c0[np.arange(25), n[c == 0]] = 1.0
    count = ((b == 0).astype(np.float32) + (b == 4) + (c == 0) + (c == 4)).reshape(1, NODES, 1)
    return west, east, take_c4, take_c0, count


def flat_gather(value, axes):
    size = value.size
    whole = lax.all_gather(value.reshape(size), axes, axis=0, tiled=True)
    return whole.reshape((-1,) + value.shape)


def far_kernels(geometry, observers):
    separation = observers[:, None, :] - geometry[:3, :, None]
    square = jnp.sum(separation * separation, axis=0)
    radius = jnp.sqrt(square)
    normal_part = jnp.sum(geometry[3:6, :, None] * separation, axis=0)
    near_kernel = (normal_part / (four_pi * square * radius)).astype(jnp.bfloat16)
    rate_kernel = (normal_part / (four_pi * square)).astype(jnp.bfloat16)
    return (near_kernel, rate_kernel)


def per_device(
    fields,
    segment_register,
    volume_operator,
    flux_jacobian,
    penalty,
    face_element,
    rotation,
    pressure_history,
    surface_geometry,
    observer_sites,
    delay_table,
):
    elements = fields.shape[2]
    face_count = face_element.shape[0]
    west_np, east_np, take_c4_np, take_c0_np, count_np = node_tables()
    west_sel = jnp.asarray(west_np)
    east_sel = jnp.asarray(east_np)
    take_c4 = jnp.asarray(take_c4_np)
    take_c0 = jnp.asarray(take_c0_np)
    weight = penalty.reshape(VARS, 1, 1)
    mesh_size = lax.axis_size("mesh")
    sect_size = lax.axis_size("sect")
    devices = mesh_size * sect_size
    my_mesh = lax.axis_index("mesh")
    my_sect = lax.axis_index("sect")

    west_part = jnp.einsum("nm,vme->vne", west_sel, fields, precision=highest_value)
    east_part = jnp.einsum("nm,vme->vne", east_sel, fields, precision=highest_value)
    forward = [(i, (i + 1) % mesh_size) for i in range(mesh_size)]
    backward = [(j, i) for i, j in forward]
    west_halo = lax.ppermute(west_part[:, :, elements - 1 :], "mesh", forward)
    east_halo = lax.ppermute(east_part[:, :, :1], "mesh", backward)
    upward = [(i, i + 1) for i in range(sect_size - 1)]
    downward = [(j, i) for i, j in upward]
    top_rows = jnp.einsum("jm,vme->vje", take_c4, fields, precision=highest_value)
    bottom_rows = jnp.einsum("jm,vme->vje", take_c0, fields, precision=highest_value)
    from_below = lax.ppermute(top_rows, "sect", upward)
    from_above = lax.ppermute(bottom_rows, "sect", downward)

    selector = (face_element[:, None] == jnp.arange(elements, dtype=jnp.int32)[None, :]).astype(
        jnp.float32
    )
    rotor_rows = jnp.einsum("vqe,fe->vqf", fields[:, 0:25], selector, precision=highest_value)
    stator = jnp.einsum("vqe,fe->vqf", fields[:, 100:125], selector, precision=highest_value)

    combined = jnp.einsum(
        "dso,dnm->snom", flux_jacobian, volume_operator, precision=highest_value
    )
    volume = jnp.einsum("snom,ome->sne", combined, fields, precision=highest_value)

    west_beyond = jnp.concatenate([west_halo, west_part[:, :, : elements - 1]], axis=2)
    east_beyond = jnp.concatenate([east_part[:, :, 1:], east_halo], axis=2)
    lower_beyond = jnp.einsum("jn,vje->vne", take_c0, from_below, precision=highest_value)
    upper_beyond = jnp.einsum("jn,vje->vne", take_c4, from_above, precision=highest_value)
    stator_lift = jnp.einsum("vqf,fe->vqe", weight * stator, selector, precision=highest_value)
    stator_full = jnp.concatenate(
        [jnp.zeros((VARS, 100, elements), jnp.float32), stator_lift], axis=1
    )
    neighbours = west_beyond + east_beyond + lower_beyond + upper_beyond
    base_tendency = volume + weight * (neighbours - jnp.asarray(count_np) * fields) - stator_full

    top_base = fields[VARS - 1, 100:125] + segment_gain * (
        segment_decay * segment_register[VARS - 1, 100:125]
        + time_step * base_tendency[VARS - 1, 100:125]
    )
    sampled = jnp.einsum("qe,fe->qf", top_base, selector, precision=highest_value)
    surface_base = jnp.mean(sampled, axis=0)
    rotor_sum = jnp.sum(rotor_rows[VARS - 1], axis=0)

    shift = rotation[0] // face_count
    within = rotation[0] % face_count
    slots = jnp.arange(face_count, dtype=jnp.int32)
    dest = jnp.arange(devices, dtype=jnp.int32)
    dest_mesh = dest // sect_size
    dest_sect = dest % sect_size
    same_sect = dest_sect == my_sect
    first = same_sect & (dest_mesh == (my_mesh - shift) % mesh_size)
    second = same_sect & (dest_mesh == (my_mesh - shift - 1) % mesh_size)
    keep = (first[:, None] & (slots >= within)[None, :]) | (
        second[:, None] & (slots < within)[None, :]
    )
    rotor_send = jnp.where(keep[:, None, None, :], rotor_rows[None], 0.0).reshape(devices, -1)
    shared = jnp.concatenate(
        [
            pressure_history.astype(jnp.float32).reshape(-1),
            surface_geometry.astype(jnp.float32).reshape(-1),
            face_element.astype(jnp.float32),
            surface_base,
            rotor_sum,
            rotation.astype(jnp.float32),
        ]
    )
    send = jnp.concatenate(
        [rotor_send, jnp.broadcast_to(shared[None], (devices, shared.shape[0]))], axis=1
    )
    recv = lax.all_to_all(send, ALL, 0, 0, tiled=True)

    rotor_width = VARS * 25 * face_count
    near_slab = (my_mesh + shift) % mesh_size
    far_slab = (near_slab + 1) % mesh_size
    arrived = (
        lax.dynamic_index_in_dim(recv, near_slab * sect_size + my_sect, 0, keepdims=False)
        + lax.dynamic_index_in_dim(recv, far_slab * sect_size + my_sect, 0, keepdims=False)
    )[:rotor_width].reshape(VARS, 25, face_count)
    order = (slots + within) % face_count
    rotated = jnp.take(arrived, order, axis=2)
    rotor_lift = jnp.einsum("vqf,fe->vqe", weight * rotated, selector, precision=highest_value)
    rotor_full = jnp.concatenate(
        [jnp.zeros((VARS, 100, elements), jnp.float32), rotor_lift], axis=1
    )
    rate_tendency = base_tendency + rotor_full
    new_register = segment_decay * segment_register + time_step * rate_tendency
    new_fields = fields + segment_gain * new_register

    info = recv[:, rotor_width:]
    hist_rows = pressure_history.shape[0]
    geo_at = hist_rows * face_count
    fe_at = geo_at + 6 * face_count
    base_at = fe_at + face_count
    sum_at = base_at + face_count
    rot_at = sum_at + face_count
    all_fe = info[:, fe_at : fe_at + face_count]
    all_base = info[:, base_at : base_at + face_count]
    all_sum = info[:, sum_at : sum_at + face_count]
    cycle = mesh_size * face_count
    by_sect = jnp.transpose(all_sum.reshape(mesh_size, sect_size, face_count), (1, 0, 2)).reshape(
        sect_size, cycle
    )
    doubled = jnp.concatenate([by_sect, by_sect], axis=1)
    rolled = jnp.stack(
        [
            lax.dynamic_slice_in_dim(doubled[k], info[k, rot_at].astype(jnp.int32) % cycle, cycle)
            for k in range(sect_size)
        ]
    )
    rolled = jnp.transpose(rolled.reshape(sect_size, mesh_size, face_count), (1, 0, 2)).reshape(
        devices, face_count
    )
    same = (all_fe[:, :, None] == all_fe[:, None, :]).astype(jnp.float32)
    rotor_part = jnp.sum(same * rolled[:, None, :], axis=2)
    gain = segment_gain * time_step * penalty[VARS - 1] / 25.0
    surface_now = (all_base + gain * rotor_part).astype(jnp.bfloat16)

    delays = delay_table[:, 0]
    running = jnp.zeros((TB, observer_sites.shape[1]), jnp.float32)
    for j in range(face_count):
        history = jnp.concatenate(
            [
                info[:, j:geo_at:face_count].astype(jnp.bfloat16),
                surface_now[:, j : j + 1],
            ],
            axis=1,
        )
        window = jnp.zeros((devices, TB + 1), jnp.bfloat16)
        for bin_ in range(NB):
            window = jnp.where(
                (delays == bin_)[:, None], history[:, NB - 1 - bin_ : NB - 1 - bin_ + TB + 1], window
            )
        window_late = window[:, 1:]
        change = (window_late.astype(jnp.float32) - window[:, :-1].astype(jnp.float32)).astype(
            jnp.bfloat16
        )
        geometry = jnp.stack(
            [info[:, geo_at + i * face_count + j] for i in range(6)]
        )
        near_kernel, rate_kernel = far_kernels(geometry, observer_sites)
        contract = (((0,), (0,)), ((), ()))
        running = running + lax.dot_general(
            window_late, near_kernel, contract, preferred_element_type=jnp.float32
        ) + lax.dot_general(change, rate_kernel, contract, preferred_element_type=jnp.float32)
    return (new_fields, new_register, running)


def solution(mesh):
    placed = (
        P(None, None, ALL),
        P(None, None, ALL),
        P(),
        P(),
        P(),
        P(ALL),
        P("sect"),
        P(None, ALL),
        P(None, ALL),
        P(None, ALL),
        P(None, ALL),
    )
    return jax.shard_map(
        per_device,
        mesh=mesh,
        in_specs=placed,
        out_specs=(
            P(None, None, ALL),
            P(None, None, ALL),
            P(None, ALL),
        ),
        check_vma=False,
    )
```

```python
import numpy as np
import jax
import jax.numpy as jnp
from jax import lax
from jax.sharding import PartitionSpec as P

VARS = 5
NODES = 125
FACE_DEV = 4
TB = 8
NB = 8

segment_decay = -0.4178904745
segment_gain = 1.4061
time_step = 0.2
four_pi = 12.566370614359172
highest_value = lax.Precision.HIGHEST
ALL = ("mesh", "sect")


def node_tables():
    a, b, c = np.meshgrid(np.arange(5), np.arange(5), np.arange(5), indexing="ij")
    a, b, c = a.reshape(-1), b.reshape(-1), c.reshape(-1)
    n = np.arange(NODES)
    west = np.zeros((NODES, NODES), np.float32)
    west[n[b == 0], n[b == 0] + 20] = 1.0
    east = np.zeros((NODES, NODES), np.float32)
    east[n[b == 4], n[b == 4] - 20] = 1.0
    take_c4 = np.zeros((25, NODES), np.float32)
    take_c4[np.arange(25), n[c == 4]] = 1.0
    take_c0 = np.zeros((25, NODES), np.float32)
    take_c0[np.arange(25), n[c == 0]] = 1.0
    count = ((b == 0).astype(np.float32) + (b == 4) + (c == 0) + (c == 4)).reshape(1, NODES, 1)
    return west, east, take_c4, take_c0, count


def flat_gather(value, axes):
    size = value.size
    whole = lax.all_gather(value.reshape(size), axes, axis=0, tiled=True)
    return whole.reshape((-1,) + value.shape)


def far_kernels(geometry, observers):
    separation = observers[:, None, :] - geometry[:3, :, None]
    square = jnp.sum(separation * separation, axis=0)
    radius = jnp.sqrt(square)
    normal_part = jnp.sum(geometry[3:6, :, None] * separation, axis=0)
    near_kernel = (normal_part / (four_pi * square * radius)).astype(jnp.bfloat16)
    rate_kernel = (normal_part / (four_pi * square)).astype(jnp.bfloat16)
    return (near_kernel, rate_kernel)


def per_device(
    fields,
    segment_register,
    volume_operator,
    flux_jacobian,
    penalty,
    face_element,
    rotation,
    pressure_history,
    surface_geometry,
    observer_sites,
    delay_table,
):
    elements = fields.shape[2]
    face_count = face_element.shape[0]
    west_np, east_np, take_c4_np, take_c0_np, count_np = node_tables()
    west_sel = jnp.asarray(west_np)
    east_sel = jnp.asarray(east_np)
    take_c4 = jnp.asarray(take_c4_np)
    take_c0 = jnp.asarray(take_c0_np)
    weight = penalty.reshape(VARS, 1, 1)
    mesh_size = lax.axis_size("mesh")
    sect_size = lax.axis_size("sect")
    devices = mesh_size * sect_size
    my_mesh = lax.axis_index("mesh")
    my_sect = lax.axis_index("sect")

    west_part = jnp.einsum("nm,vme->vne", west_sel, fields, precision=highest_value)
    east_part = jnp.einsum("nm,vme->vne", east_sel, fields, precision=highest_value)
    forward = [(i, (i + 1) % mesh_size) for i in range(mesh_size)]
    backward = [(j, i) for i, j in forward]
    west_halo = lax.ppermute(west_part[:, :, elements - 1 :], "mesh", forward)
    east_halo = lax.ppermute(east_part[:, :, :1], "mesh", backward)
    upward = [(i, i + 1) for i in range(sect_size - 1)]
    downward = [(j, i) for i, j in upward]
    top_rows = jnp.einsum("jm,vme->vje", take_c4, fields, precision=highest_value)
    bottom_rows = jnp.einsum("jm,vme->vje", take_c0, fields, precision=highest_value)
    from_below = lax.ppermute(top_rows, "sect", upward)
    from_above = lax.ppermute(bottom_rows, "sect", downward)

    selector = (face_element[:, None] == jnp.arange(elements, dtype=jnp.int32)[None, :]).astype(
        jnp.float32
    )
    rotor_rows = jnp.einsum("vqe,fe->vqf", fields[:, 0:25], selector, precision=highest_value)
    stator = jnp.einsum("vqe,fe->vqf", fields[:, 100:125], selector, precision=highest_value)

    combined = jnp.einsum(
        "dso,dnm->snom", flux_jacobian, volume_operator, precision=highest_value
    )
    volume = jnp.einsum("snom,ome->sne", combined, fields, precision=highest_value)

    west_beyond = jnp.concatenate([west_halo, west_part[:, :, : elements - 1]], axis=2)
    east_beyond = jnp.concatenate([east_part[:, :, 1:], east_halo], axis=2)
    lower_beyond = jnp.einsum("jn,vje->vne", take_c0, from_below, precision=highest_value)
    upper_beyond = jnp.einsum("jn,vje->vne", take_c4, from_above, precision=highest_value)
    stator_lift = jnp.einsum("vqf,fe->vqe", weight * stator, selector, precision=highest_value)
    stator_full = jnp.concatenate(
        [jnp.zeros((VARS, 100, elements), jnp.float32), stator_lift], axis=1
    )
    neighbours = west_beyond + east_beyond + lower_beyond + upper_beyond
    base_tendency = volume + weight * (neighbours - jnp.asarray(count_np) * fields) - stator_full

    element_ids = jnp.arange(elements, dtype=jnp.int32)[None, :]
    before = ((face_element - 1)[:, None] == element_ids).astype(jnp.float32)
    after = ((face_element + 1)[:, None] == element_ids).astype(jnp.float32)
    at_first = (face_element == 0).astype(jnp.float32)
    at_last = (face_element == elements - 1).astype(jnp.float32)
    columns = jnp.einsum("vme,fe->vmf", fields, selector, precision=highest_value)
    columns_before = jnp.einsum("vme,fe->vmf", fields, before, precision=highest_value)
    columns_after = jnp.einsum("vme,fe->vmf", fields, after, precision=highest_value)
    top = slice(100, 125)
    west_col = jnp.einsum(
        "nm,vmf->vnf", west_sel[top], columns_before, precision=highest_value
    ) + west_halo[:, top] * at_first
    east_col = jnp.einsum(
        "nm,vmf->vnf", east_sel[top], columns_after, precision=highest_value
    ) + east_halo[:, top] * at_last
    lower_col = jnp.einsum(
        "jn,vjf->vnf",
        take_c0[:, top],
        jnp.einsum("vje,fe->vjf", from_below, selector, precision=highest_value),
        precision=highest_value,
    )
    upper_col = jnp.einsum(
        "jn,vjf->vnf",
        take_c4[:, top],
        jnp.einsum("vje,fe->vjf", from_above, selector, precision=highest_value),
        precision=highest_value,
    )
    volume_col = jnp.einsum(
        "snom,omf->snf", combined[:, top], columns, precision=highest_value
    )
    same_face = (face_element[:, None] == face_element[None, :]).astype(jnp.float32)
    stator_col = jnp.einsum("vqf,gf->vqg", weight * stator, same_face, precision=highest_value)
    base_col = (
        volume_col
        + weight * (west_col + east_col + lower_col + upper_col - jnp.asarray(count_np)[:, top] * columns[:, top])
        - stator_col
    )
    register_col = jnp.einsum(
        "qe,fe->qf", segment_register[VARS - 1, 100:125], selector, precision=highest_value
    )
    top_base = columns[VARS - 1, top] + segment_gain * (
        segment_decay * register_col + time_step * base_col[VARS - 1]
    )
    surface_base = jnp.mean(top_base, axis=0)
    rotor_sum = jnp.sum(rotor_rows[VARS - 1], axis=0)

    shift = rotation[0] // face_count
    within = rotation[0] % face_count
    slots = jnp.arange(face_count, dtype=jnp.int32)
    dest = jnp.arange(devices, dtype=jnp.int32)
    dest_mesh = dest // sect_size
    dest_sect = dest % sect_size
    same_sect = dest_sect == my_sect
    first = same_sect & (dest_mesh == (my_mesh - shift) % mesh_size)
    second = same_sect & (dest_mesh == (my_mesh - shift - 1) % mesh_size)
    keep = (first[:, None] & (slots >= within)[None, :]) | (
        second[:, None] & (slots < within)[None, :]
    )
    rotor_send = jnp.where(keep[:, None, None, :], rotor_rows[None], 0.0).reshape(devices, -1)
    shared = jnp.concatenate(
        [
            pressure_history.astype(jnp.float32).reshape(-1),
            surface_geometry.astype(jnp.float32).reshape(-1),
            face_element.astype(jnp.float32),
            surface_base,
            rotor_sum,
            rotation.astype(jnp.float32),
        ]
    )
    send = jnp.concatenate(
        [rotor_send, jnp.broadcast_to(shared[None], (devices, shared.shape[0]))], axis=1
    )
    recv = lax.all_to_all(send, ALL, 0, 0, tiled=True)

    rotor_width = VARS * 25 * face_count
    near_slab = (my_mesh + shift) % mesh_size
    far_slab = (near_slab + 1) % mesh_size
    arrived = (
        lax.dynamic_index_in_dim(recv, near_slab * sect_size + my_sect, 0, keepdims=False)
        + lax.dynamic_index_in_dim(recv, far_slab * sect_size + my_sect, 0, keepdims=False)
    )[:rotor_width].reshape(VARS, 25, face_count)
    order = (slots + within) % face_count
    rotated = jnp.take(arrived, order, axis=2)
    rotor_lift = jnp.einsum("vqf,fe->vqe", weight * rotated, selector, precision=highest_value)
    rotor_full = jnp.concatenate(
        [jnp.zeros((VARS, 100, elements), jnp.float32), rotor_lift], axis=1
    )
    rate_tendency = base_tendency + rotor_full
    new_register = segment_decay * segment_register + time_step * rate_tendency
    new_fields = fields + segment_gain * new_register

    info = recv[:, rotor_width:]
    hist_rows = pressure_history.shape[0]
    geo_at = hist_rows * face_count
    fe_at = geo_at + 6 * face_count
    base_at = fe_at + face_count
    sum_at = base_at + face_count
    rot_at = sum_at + face_count
    all_fe = info[:, fe_at : fe_at + face_count]
    all_base = info[:, base_at : base_at + face_count]
    all_sum = info[:, sum_at : sum_at + face_count]
    cycle = mesh_size * face_count
    by_sect = jnp.transpose(all_sum.reshape(mesh_size, sect_size, face_count), (1, 0, 2)).reshape(
        sect_size, cycle
    )
    doubled = jnp.concatenate([by_sect, by_sect], axis=1)
    rolled = jnp.stack(
        [
            lax.dynamic_slice_in_dim(doubled[k], info[k, rot_at].astype(jnp.int32) % cycle, cycle)
            for k in range(sect_size)
        ]
    )
    rolled = jnp.transpose(rolled.reshape(sect_size, mesh_size, face_count), (1, 0, 2)).reshape(
        devices, face_count
    )
    same = (all_fe[:, :, None] == all_fe[:, None, :]).astype(jnp.float32)
    rotor_part = jnp.sum(same * rolled[:, None, :], axis=2)
    gain = segment_gain * time_step * penalty[VARS - 1] / 25.0
    surface_now = (all_base + gain * rotor_part).astype(jnp.bfloat16)

    delays = delay_table[:, 0]
    running = jnp.zeros((TB, observer_sites.shape[1]), jnp.float32)
    for j in range(face_count):
        history = jnp.concatenate(
            [
                info[:, j:geo_at:face_count].astype(jnp.bfloat16),
                surface_now[:, j : j + 1],
            ],
            axis=1,
        )
        window = jnp.zeros((devices, TB + 1), jnp.bfloat16)
        for bin_ in range(NB):
            window = jnp.where(
                (delays == bin_)[:, None], history[:, NB - 1 - bin_ : NB - 1 - bin_ + TB + 1], window
            )
        window_late = window[:, 1:]
        change = (window_late.astype(jnp.float32) - window[:, :-1].astype(jnp.float32)).astype(
            jnp.bfloat16
        )
        geometry = jnp.stack(
            [info[:, geo_at + i * face_count + j] for i in range(6)]
        )
        near_kernel, rate_kernel = far_kernels(geometry, observer_sites)
        contract = (((0,), (0,)), ((), ()))
        running = running + lax.dot_general(
            window_late, near_kernel, contract, preferred_element_type=jnp.float32
        ) + lax.dot_general(change, rate_kernel, contract, preferred_element_type=jnp.float32)
    return (new_fields, new_register, running)


def solution(mesh):
    placed = (
        P(None, None, ALL),
        P(None, None, ALL),
        P(),
        P(),
        P(),
        P(ALL),
        P("sect"),
        P(None, ALL),
        P(None, ALL),
        P(None, ALL),
        P(None, ALL),
    )
    return jax.shard_map(
        per_device,
        mesh=mesh,
        in_specs=placed,
        out_specs=(
            P(None, None, ALL),
            P(None, None, ALL),
            P(None, ALL),
        ),
        check_vma=False,
    )
```

```python
import numpy as np
import jax
import jax.numpy as jnp
from jax import lax
from jax.sharding import PartitionSpec as P

VARS = 5
NODES = 125
FACE_DEV = 4
TB = 8
NB = 8

segment_decay = -0.4178904745
segment_gain = 1.4061
time_step = 0.2
four_pi = 12.566370614359172
highest_value = lax.Precision.HIGHEST
ALL = ("mesh", "sect")


def node_tables():
    a, b, c = np.meshgrid(np.arange(5), np.arange(5), np.arange(5), indexing="ij")
    a, b, c = a.reshape(-1), b.reshape(-1), c.reshape(-1)
    n = np.arange(NODES)
    west = np.zeros((NODES, NODES), np.float32)
    west[n[b == 0], n[b == 0] + 20] = 1.0
    east = np.zeros((NODES, NODES), np.float32)
    east[n[b == 4], n[b == 4] - 20] = 1.0
    take_c4 = np.zeros((25, NODES), np.float32)
    take_c4[np.arange(25), n[c == 4]] = 1.0
    take_c0 = np.zeros((25, NODES), np.float32)
    take_c0[np.arange(25), n[c == 0]] = 1.0
    count = ((b == 0).astype(np.float32) + (b == 4) + (c == 0) + (c == 4)).reshape(1, NODES, 1)
    return west, east, take_c4, take_c0, count


def flat_gather(value, axes):
    size = value.size
    whole = lax.all_gather(value.reshape(size), axes, axis=0, tiled=True)
    return whole.reshape((-1,) + value.shape)


def far_kernels(geometry, observers):
    separation = observers[:, None, :] - geometry[:3, :, None]
    square = jnp.sum(separation * separation, axis=0)
    radius = jnp.sqrt(square)
    normal_part = jnp.sum(geometry[3:6, :, None] * separation, axis=0)
    near_kernel = (normal_part / (four_pi * square * radius)).astype(jnp.bfloat16)
    rate_kernel = (normal_part / (four_pi * square)).astype(jnp.bfloat16)
    return (near_kernel, rate_kernel)


def per_device(
    fields,
    segment_register,
    volume_operator,
    flux_jacobian,
    penalty,
    face_element,
    rotation,
    pressure_history,
    surface_geometry,
    observer_sites,
    delay_table,
):
    elements = fields.shape[2]
    face_count = face_element.shape[0]
    west_np, east_np, take_c4_np, take_c0_np, count_np = node_tables()
    west_sel = jnp.asarray(west_np)
    east_sel = jnp.asarray(east_np)
    take_c4 = jnp.asarray(take_c4_np)
    take_c0 = jnp.asarray(take_c0_np)
    weight = penalty.reshape(VARS, 1, 1)
    mesh_size = lax.axis_size("mesh")
    sect_size = lax.axis_size("sect")
    devices = mesh_size * sect_size
    my_mesh = lax.axis_index("mesh")
    my_sect = lax.axis_index("sect")

    west_part = jnp.einsum("nm,vme->vne", west_sel, fields, precision=highest_value)
    east_part = jnp.einsum("nm,vme->vne", east_sel, fields, precision=highest_value)
    forward = [(i, (i + 1) % mesh_size) for i in range(mesh_size)]
    backward = [(j, i) for i, j in forward]
    west_halo = lax.ppermute(west_part[:, :, elements - 1 :], "mesh", forward)
    east_halo = lax.ppermute(east_part[:, :, :1], "mesh", backward)
    upward = [(i, i + 1) for i in range(sect_size - 1)]
    downward = [(j, i) for i, j in upward]
    top_rows = jnp.einsum("jm,vme->vje", take_c4, fields, precision=highest_value)
    bottom_rows = jnp.einsum("jm,vme->vje", take_c0, fields, precision=highest_value)
    from_below = lax.ppermute(top_rows, "sect", upward)
    from_above = lax.ppermute(bottom_rows, "sect", downward)

    selector = (face_element[:, None] == jnp.arange(elements, dtype=jnp.int32)[None, :]).astype(
        jnp.float32
    )
    rotor_rows = jnp.einsum("vqe,fe->vqf", fields[:, 0:25], selector, precision=highest_value)
    stator = jnp.einsum("vqe,fe->vqf", fields[:, 100:125], selector, precision=highest_value)

    combined = jnp.einsum(
        "dso,dnm->snom", flux_jacobian, volume_operator, precision=highest_value
    )
    volume = jnp.einsum("snom,ome->sne", combined, fields, precision=highest_value)

    west_beyond = jnp.concatenate([west_halo, west_part[:, :, : elements - 1]], axis=2)
    east_beyond = jnp.concatenate([east_part[:, :, 1:], east_halo], axis=2)
    lower_beyond = jnp.einsum("jn,vje->vne", take_c0, from_below, precision=highest_value)
    upper_beyond = jnp.einsum("jn,vje->vne", take_c4, from_above, precision=highest_value)
    stator_lift = jnp.einsum("vqf,fe->vqe", weight * stator, selector, precision=highest_value)
    stator_full = jnp.concatenate(
        [jnp.zeros((VARS, 100, elements), jnp.float32), stator_lift], axis=1
    )
    neighbours = west_beyond + east_beyond + lower_beyond + upper_beyond
    base_tendency = volume + weight * (neighbours - jnp.asarray(count_np) * fields) - stator_full

    element_ids = jnp.arange(elements, dtype=jnp.int32)[None, :]
    before = ((face_element - 1)[:, None] == element_ids).astype(jnp.float32)
    after = ((face_element + 1)[:, None] == element_ids).astype(jnp.float32)
    at_first = (face_element == 0).astype(jnp.float32)
    at_last = (face_element == elements - 1).astype(jnp.float32)
    columns = jnp.einsum("vme,fe->vmf", fields, selector, precision=highest_value)
    columns_before = jnp.einsum("vme,fe->vmf", fields, before, precision=highest_value)
    columns_after = jnp.einsum("vme,fe->vmf", fields, after, precision=highest_value)
    top = slice(100, 125)
    west_col = jnp.einsum(
        "nm,vmf->vnf", west_sel[top], columns_before, precision=highest_value
    ) + west_halo[:, top] * at_first
    east_col = jnp.einsum(
        "nm,vmf->vnf", east_sel[top], columns_after, precision=highest_value
    ) + east_halo[:, top] * at_last
    lower_col = jnp.einsum(
        "jn,vjf->vnf",
        take_c0[:, top],
        jnp.einsum("vje,fe->vjf", from_below, selector, precision=highest_value),
        precision=highest_value,
    )
    upper_col = jnp.einsum(
        "jn,vjf->vnf",
        take_c4[:, top],
        jnp.einsum("vje,fe->vjf", from_above, selector, precision=highest_value),
        precision=highest_value,
    )
    volume_col = jnp.einsum(
        "snom,omf->snf", combined[:, top], columns, precision=highest_value
    )
    same_face = (face_element[:, None] == face_element[None, :]).astype(jnp.float32)
    stator_col = jnp.einsum("vqf,gf->vqg", weight * stator, same_face, precision=highest_value)
    base_col = (
        volume_col
        + weight * (west_col + east_col + lower_col + upper_col - jnp.asarray(count_np)[:, top] * columns[:, top])
        - stator_col
    )
    register_col = jnp.einsum(
        "qe,fe->qf", segment_register[VARS - 1, 100:125], selector, precision=highest_value
    )
    top_base = columns[VARS - 1, top] + segment_gain * (
        segment_decay * register_col + time_step * base_col[VARS - 1]
    )
    surface_base = jnp.mean(top_base, axis=0)
    rotor_sum = jnp.sum(rotor_rows[VARS - 1], axis=0)

    shift = rotation[0] // face_count
    within = rotation[0] % face_count
    slots = jnp.arange(face_count, dtype=jnp.int32)
    dest_mesh = jnp.arange(mesh_size, dtype=jnp.int32)
    first = dest_mesh == (my_mesh - shift) % mesh_size
    second = dest_mesh == (my_mesh - shift - 1) % mesh_size
    keep = (first[:, None] & (slots >= within)[None, :]) | (
        second[:, None] & (slots < within)[None, :]
    )
    rotor_send = jnp.where(keep[:, None, None, :], rotor_rows[None], 0.0).reshape(mesh_size, -1)
    shared = jnp.concatenate(
        [
            pressure_history.astype(jnp.float32).reshape(-1),
            surface_geometry.astype(jnp.float32).reshape(-1),
            face_element.astype(jnp.float32),
            surface_base,
            rotor_sum,
            rotation.astype(jnp.float32),
        ]
    )
    shared_sect = lax.all_gather(shared[None], "sect", axis=0, tiled=True).reshape(-1)
    send = jnp.concatenate(
        [rotor_send, jnp.broadcast_to(shared_sect[None], (mesh_size, shared_sect.shape[0]))],
        axis=1,
    )
    recv = lax.all_to_all(send, "mesh", 0, 0, tiled=True)

    rotor_width = VARS * 25 * face_count
    near_slab = (my_mesh + shift) % mesh_size
    far_slab = (near_slab + 1) % mesh_size
    arrived = (
        lax.dynamic_index_in_dim(recv, near_slab, 0, keepdims=False)
        + lax.dynamic_index_in_dim(recv, far_slab, 0, keepdims=False)
    )[:rotor_width].reshape(VARS, 25, face_count)
    order = (slots + within) % face_count
    rotated = jnp.take(arrived, order, axis=2)
    rotor_lift = jnp.einsum("vqf,fe->vqe", weight * rotated, selector, precision=highest_value)
    rotor_full = jnp.concatenate(
        [jnp.zeros((VARS, 100, elements), jnp.float32), rotor_lift], axis=1
    )
    rate_tendency = base_tendency + rotor_full
    new_register = segment_decay * segment_register + time_step * rate_tendency
    new_fields = fields + segment_gain * new_register

    info = recv[:, rotor_width:].reshape(devices, shared.shape[0])
    hist_rows = pressure_history.shape[0]
    geo_at = hist_rows * face_count
    fe_at = geo_at + 6 * face_count
    base_at = fe_at + face_count
    sum_at = base_at + face_count
    rot_at = sum_at + face_count
    all_fe = info[:, fe_at : fe_at + face_count]
    all_base = info[:, base_at : base_at + face_count]
    all_sum = info[:, sum_at : sum_at + face_count]
    cycle = mesh_size * face_count
    by_sect = jnp.transpose(all_sum.reshape(mesh_size, sect_size, face_count), (1, 0, 2)).reshape(
        sect_size, cycle
    )
    doubled = jnp.concatenate([by_sect, by_sect], axis=1)
    rolled = jnp.stack(
        [
            lax.dynamic_slice_in_dim(doubled[k], info[k, rot_at].astype(jnp.int32) % cycle, cycle)
            for k in range(sect_size)
        ]
    )
    rolled = jnp.transpose(rolled.reshape(sect_size, mesh_size, face_count), (1, 0, 2)).reshape(
        devices, face_count
    )
    same = (all_fe[:, :, None] == all_fe[:, None, :]).astype(jnp.float32)
    rotor_part = jnp.sum(same * rolled[:, None, :], axis=2)
    gain = segment_gain * time_step * penalty[VARS - 1] / 25.0
    surface_now = (all_base + gain * rotor_part).astype(jnp.bfloat16)

    delays = delay_table[:, 0]
    running = jnp.zeros((TB, observer_sites.shape[1]), jnp.float32)
    for j in range(face_count):
        history = jnp.concatenate(
            [
                info[:, j:geo_at:face_count].astype(jnp.bfloat16),
                surface_now[:, j : j + 1],
            ],
            axis=1,
        )
        window = jnp.zeros((devices, TB + 1), jnp.bfloat16)
        for bin_ in range(NB):
            window = jnp.where(
                (delays == bin_)[:, None], history[:, NB - 1 - bin_ : NB - 1 - bin_ + TB + 1], window
            )
        window_late = window[:, 1:]
        change = (window_late.astype(jnp.float32) - window[:, :-1].astype(jnp.float32)).astype(
            jnp.bfloat16
        )
        geometry = jnp.stack(
            [info[:, geo_at + i * face_count + j] for i in range(6)]
        )
        near_kernel, rate_kernel = far_kernels(geometry, observer_sites)
        contract = (((0,), (0,)), ((), ()))
        running = running + lax.dot_general(
            window_late, near_kernel, contract, preferred_element_type=jnp.float32
        ) + lax.dot_general(change, rate_kernel, contract, preferred_element_type=jnp.float32)
    return (new_fields, new_register, running)


def solution(mesh):
    placed = (
        P(None, None, ALL),
        P(None, None, ALL),
        P(),
        P(),
        P(),
        P(ALL),
        P("sect"),
        P(None, ALL),
        P(None, ALL),
        P(None, ALL),
        P(None, ALL),
    )
    return jax.shard_map(
        per_device,
        mesh=mesh,
        in_specs=placed,
        out_specs=(
            P(None, None, ALL),
            P(None, None, ALL),
            P(None, ALL),
        ),
        check_vma=False,
    )
```

```python
import numpy as np
import jax
import jax.numpy as jnp
from jax import lax
from jax.sharding import PartitionSpec as P

VARS = 5
NODES = 125
FACE_DEV = 4
TB = 8
NB = 8

segment_decay = -0.4178904745
segment_gain = 1.4061
time_step = 0.2
four_pi = 12.566370614359172
highest_value = lax.Precision.HIGHEST
ALL = ("mesh", "sect")


def node_tables():
    a, b, c = np.meshgrid(np.arange(5), np.arange(5), np.arange(5), indexing="ij")
    a, b, c = a.reshape(-1), b.reshape(-1), c.reshape(-1)
    n = np.arange(NODES)
    west = np.zeros((NODES, NODES), np.float32)
    west[n[b == 0], n[b == 0] + 20] = 1.0
    east = np.zeros((NODES, NODES), np.float32)
    east[n[b == 4], n[b == 4] - 20] = 1.0
    take_c4 = np.zeros((25, NODES), np.float32)
    take_c4[np.arange(25), n[c == 4]] = 1.0
    take_c0 = np.zeros((25, NODES), np.float32)
    take_c0[np.arange(25), n[c == 0]] = 1.0
    count = ((b == 0).astype(np.float32) + (b == 4) + (c == 0) + (c == 4)).reshape(1, NODES, 1)
    return west, east, take_c4, take_c0, count


def flat_gather(value, axes):
    size = value.size
    whole = lax.all_gather(value.reshape(size), axes, axis=0, tiled=True)
    return whole.reshape((-1,) + value.shape)


def far_kernels(geometry, observers):
    separation = observers[:, None, :] - geometry[:3, :, None]
    square = jnp.sum(separation * separation, axis=0)
    radius = jnp.sqrt(square)
    normal_part = jnp.sum(geometry[3:6, :, None] * separation, axis=0)
    near_kernel = (normal_part / (four_pi * square * radius)).astype(jnp.bfloat16)
    rate_kernel = (normal_part / (four_pi * square)).astype(jnp.bfloat16)
    return (near_kernel, rate_kernel)


def per_device(
    fields,
    segment_register,
    volume_operator,
    flux_jacobian,
    penalty,
    face_element,
    rotation,
    pressure_history,
    surface_geometry,
    observer_sites,
    delay_table,
):
    elements = fields.shape[2]
    face_count = face_element.shape[0]
    west_np, east_np, take_c4_np, take_c0_np, count_np = node_tables()
    west_sel = jnp.asarray(west_np)
    east_sel = jnp.asarray(east_np)
    take_c4 = jnp.asarray(take_c4_np)
    take_c0 = jnp.asarray(take_c0_np)
    weight = penalty.reshape(VARS, 1, 1)
    mesh_size = lax.axis_size("mesh")
    sect_size = lax.axis_size("sect")
    devices = mesh_size * sect_size
    my_mesh = lax.axis_index("mesh")
    my_sect = lax.axis_index("sect")

    forward = [(i, (i + 1) % mesh_size) for i in range(mesh_size)]
    backward = [(j, i) for i, j in forward]
    west_send = jnp.einsum(
        "nm,vme->vne", west_sel, fields[:, :, elements - 1 :], precision=highest_value
    )
    east_send = jnp.einsum("nm,vme->vne", east_sel, fields[:, :, :1], precision=highest_value)
    west_halo = lax.ppermute(west_send, "mesh", forward)
    east_halo = lax.ppermute(east_send, "mesh", backward)
    upward = [(i, i + 1) for i in range(sect_size - 1)]
    downward = [(j, i) for i, j in upward]
    top_rows = fields[:, 4::5]
    bottom_rows = fields[:, 0::5]
    from_below = lax.ppermute(top_rows, "sect", upward)
    from_above = lax.ppermute(bottom_rows, "sect", downward)

    selector = (face_element[:, None] == jnp.arange(elements, dtype=jnp.int32)[None, :]).astype(
        jnp.float32
    )
    rotor_rows = jnp.einsum("vqe,fe->vqf", fields[:, 0:25], selector, precision=highest_value)
    stator = jnp.einsum("vqe,fe->vqf", fields[:, 100:125], selector, precision=highest_value)

    combined = jnp.einsum(
        "dso,dnm->snom", flux_jacobian, volume_operator, precision=highest_value
    )
    volume = jnp.einsum("snom,ome->sne", combined, fields, precision=highest_value)

    west_part = jnp.einsum("nm,vme->vne", west_sel, fields, precision=highest_value)
    east_part = jnp.einsum("nm,vme->vne", east_sel, fields, precision=highest_value)
    west_beyond = jnp.concatenate([west_halo, west_part[:, :, : elements - 1]], axis=2)
    east_beyond = jnp.concatenate([east_part[:, :, 1:], east_halo], axis=2)
    lower_beyond = jnp.einsum("jn,vje->vne", take_c0, from_below, precision=highest_value)
    upper_beyond = jnp.einsum("jn,vje->vne", take_c4, from_above, precision=highest_value)
    stator_lift = jnp.einsum("vqf,fe->vqe", weight * stator, selector, precision=highest_value)
    stator_full = jnp.concatenate(
        [jnp.zeros((VARS, 100, elements), jnp.float32), stator_lift], axis=1
    )
    neighbours = west_beyond + east_beyond + lower_beyond + upper_beyond
    base_tendency = volume + weight * (neighbours - jnp.asarray(count_np) * fields) - stator_full

    element_ids = jnp.arange(elements, dtype=jnp.int32)[None, :]
    before = ((face_element - 1)[:, None] == element_ids).astype(jnp.float32)
    after = ((face_element + 1)[:, None] == element_ids).astype(jnp.float32)
    at_first = (face_element == 0).astype(jnp.float32)
    at_last = (face_element == elements - 1).astype(jnp.float32)
    columns = jnp.einsum("vme,fe->vmf", fields, selector, precision=highest_value)
    columns_before = jnp.einsum("vme,fe->vmf", fields, before, precision=highest_value)
    columns_after = jnp.einsum("vme,fe->vmf", fields, after, precision=highest_value)
    top = slice(100, 125)
    west_col = jnp.einsum(
        "nm,vmf->vnf", west_sel[top], columns_before, precision=highest_value
    ) + west_halo[:, top] * at_first
    east_col = jnp.einsum(
        "nm,vmf->vnf", east_sel[top], columns_after, precision=highest_value
    ) + east_halo[:, top] * at_last
    lower_col = jnp.einsum(
        "jn,vjf->vnf",
        take_c0[:, top],
        jnp.einsum("vje,fe->vjf", from_below, selector, precision=highest_value),
        precision=highest_value,
    )
    upper_col = jnp.einsum(
        "jn,vjf->vnf",
        take_c4[:, top],
        jnp.einsum("vje,fe->vjf", from_above, selector, precision=highest_value),
        precision=highest_value,
    )
    volume_col = jnp.einsum(
        "snom,omf->snf", combined[:, top], columns, precision=highest_value
    )
    same_face = (face_element[:, None] == face_element[None, :]).astype(jnp.float32)
    stator_col = jnp.einsum("vqf,gf->vqg", weight * stator, same_face, precision=highest_value)
    base_col = (
        volume_col
        + weight * (west_col + east_col + lower_col + upper_col - jnp.asarray(count_np)[:, top] * columns[:, top])
        - stator_col
    )
    register_col = jnp.einsum(
        "qe,fe->qf", segment_register[VARS - 1, 100:125], selector, precision=highest_value
    )
    top_base = columns[VARS - 1, top] + segment_gain * (
        segment_decay * register_col + time_step * base_col[VARS - 1]
    )
    surface_base = jnp.mean(top_base, axis=0)
    rotor_sum = jnp.sum(rotor_rows[VARS - 1], axis=0)

    shift = rotation[0] // face_count
    within = rotation[0] % face_count
    slots = jnp.arange(face_count, dtype=jnp.int32)
    dest_mesh = jnp.arange(mesh_size, dtype=jnp.int32)
    first = dest_mesh == (my_mesh - shift) % mesh_size
    second = dest_mesh == (my_mesh - shift - 1) % mesh_size
    keep = (first[:, None] & (slots >= within)[None, :]) | (
        second[:, None] & (slots < within)[None, :]
    )
    rotor_send = jnp.where(keep[:, None, None, :], rotor_rows[None], 0.0).reshape(mesh_size, -1)
    shared = jnp.concatenate(
        [
            pressure_history.astype(jnp.float32).reshape(-1),
            surface_geometry.astype(jnp.float32).reshape(-1),
            face_element.astype(jnp.float32),
            surface_base,
            rotor_sum,
            rotation.astype(jnp.float32),
        ]
    )
    shared_sect = lax.all_gather(shared[None], "sect", axis=0, tiled=True).reshape(-1)
    send = jnp.concatenate(
        [rotor_send, jnp.broadcast_to(shared_sect[None], (mesh_size, shared_sect.shape[0]))],
        axis=1,
    )
    recv = lax.all_to_all(send, "mesh", 0, 0, tiled=True)

    rotor_width = VARS * 25 * face_count
    near_slab = (my_mesh + shift) % mesh_size
    far_slab = (near_slab + 1) % mesh_size
    arrived = (
        lax.dynamic_index_in_dim(recv, near_slab, 0, keepdims=False)
        + lax.dynamic_index_in_dim(recv, far_slab, 0, keepdims=False)
    )[:rotor_width].reshape(VARS, 25, face_count)
    order = (slots + within) % face_count
    rotated = jnp.take(arrived, order, axis=2)
    rotor_lift = jnp.einsum("vqf,fe->vqe", weight * rotated, selector, precision=highest_value)
    rotor_full = jnp.concatenate(
        [jnp.zeros((VARS, 100, elements), jnp.float32), rotor_lift], axis=1
    )
    rate_tendency = base_tendency + rotor_full
    new_register = segment_decay * segment_register + time_step * rate_tendency
    new_fields = fields + segment_gain * new_register

    info = recv[:, rotor_width:].reshape(devices, shared.shape[0])
    rows = jnp.transpose(info)
    hist_rows = pressure_history.shape[0]
    geo_at = hist_rows * face_count
    fe_at = geo_at + 6 * face_count
    base_at = fe_at + face_count
    sum_at = base_at + face_count
    rot_at = sum_at + face_count
    all_fe = rows[fe_at : fe_at + face_count]
    all_base = rows[base_at : base_at + face_count]
    all_sum = info[:, sum_at : sum_at + face_count]
    cycle = mesh_size * face_count
    by_sect = jnp.transpose(all_sum.reshape(mesh_size, sect_size, face_count), (1, 0, 2)).reshape(
        sect_size, cycle
    )
    doubled = jnp.concatenate([by_sect, by_sect], axis=1)
    rolled = jnp.stack(
        [
            lax.dynamic_slice_in_dim(doubled[k], info[k, rot_at].astype(jnp.int32) % cycle, cycle)
            for k in range(sect_size)
        ]
    )
    rolled = jnp.transpose(rolled.reshape(sect_size, mesh_size, face_count), (2, 1, 0)).reshape(
        face_count, devices
    )
    same = (all_fe[:, None, :] == all_fe[None, :, :]).astype(jnp.float32)
    rotor_part = jnp.sum(same * rolled[None, :, :], axis=1)
    gain = segment_gain * time_step * penalty[VARS - 1] / 25.0
    surface_now = (all_base + gain * rotor_part).astype(jnp.bfloat16)

    delays = delay_table[:, 0][None, :]
    running = jnp.zeros((TB, observer_sites.shape[1]), jnp.float32)
    for j in range(face_count):
        history = jnp.concatenate(
            [rows[j:geo_at:face_count].astype(jnp.bfloat16), surface_now[j : j + 1]], axis=0
        )
        window = jnp.zeros((TB + 1, devices), jnp.bfloat16)
        for bin_ in range(NB):
            window = jnp.where(
                delays == bin_, history[NB - 1 - bin_ : NB - 1 - bin_ + TB + 1], window
            )
        window_late = window[1:]
        change = (window_late.astype(jnp.float32) - window[:-1].astype(jnp.float32)).astype(
            jnp.bfloat16
        )
        geometry = jnp.stack([info[:, geo_at + i * face_count + j] for i in range(6)])
        near_kernel, rate_kernel = far_kernels(geometry, observer_sites)
        running = running + jnp.dot(
            window_late, near_kernel, preferred_element_type=jnp.float32
        ) + jnp.dot(change, rate_kernel, preferred_element_type=jnp.float32)
    return (new_fields, new_register, running)


def solution(mesh):
    placed = (
        P(None, None, ALL),
        P(None, None, ALL),
        P(),
        P(),
        P(),
        P(ALL),
        P("sect"),
        P(None, ALL),
        P(None, ALL),
        P(None, ALL),
        P(None, ALL),
    )
    return jax.shard_map(
        per_device,
        mesh=mesh,
        in_specs=placed,
        out_specs=(
            P(None, None, ALL),
            P(None, None, ALL),
            P(None, ALL),
        ),
        check_vma=False,
    )
```

```python
import numpy as np
import jax
import jax.numpy as jnp
from jax import lax
from jax.sharding import PartitionSpec as P

VARS = 5
NODES = 125
FACE_DEV = 4
TB = 8
NB = 8

segment_decay = -0.4178904745
segment_gain = 1.4061
time_step = 0.2
four_pi = 12.566370614359172
highest_value = lax.Precision.HIGHEST
ALL = ("mesh", "sect")


def node_tables():
    a, b, c = np.meshgrid(np.arange(5), np.arange(5), np.arange(5), indexing="ij")
    a, b, c = a.reshape(-1), b.reshape(-1), c.reshape(-1)
    n = np.arange(NODES)
    west = np.zeros((NODES, NODES), np.float32)
    west[n[b == 0], n[b == 0] + 20] = 1.0
    east = np.zeros((NODES, NODES), np.float32)
    east[n[b == 4], n[b == 4] - 20] = 1.0
    take_c4 = np.zeros((25, NODES), np.float32)
    take_c4[np.arange(25), n[c == 4]] = 1.0
    take_c0 = np.zeros((25, NODES), np.float32)
    take_c0[np.arange(25), n[c == 0]] = 1.0
    count = ((b == 0).astype(np.float32) + (b == 4) + (c == 0) + (c == 4)).reshape(1, NODES, 1)
    return west, east, take_c4, take_c0, count


def flat_gather(value, axes):
    size = value.size
    whole = lax.all_gather(value.reshape(size), axes, axis=0, tiled=True)
    return whole.reshape((-1,) + value.shape)


def far_kernels(geometry, observers):
    separation = observers[:, None, :] - geometry[:3, :, None]
    square = jnp.sum(separation * separation, axis=0)
    radius = jnp.sqrt(square)
    normal_part = jnp.sum(geometry[3:6, :, None] * separation, axis=0)
    near_kernel = (normal_part / (four_pi * square * radius)).astype(jnp.bfloat16)
    rate_kernel = (normal_part / (four_pi * square)).astype(jnp.bfloat16)
    return (near_kernel, rate_kernel)


def per_device(
    fields,
    segment_register,
    volume_operator,
    flux_jacobian,
    penalty,
    face_element,
    rotation,
    pressure_history,
    surface_geometry,
    observer_sites,
    delay_table,
):
    elements = fields.shape[2]
    face_count = face_element.shape[0]
    west_np, east_np, take_c4_np, take_c0_np, count_np = node_tables()
    west_sel = jnp.asarray(west_np)
    east_sel = jnp.asarray(east_np)
    take_c4 = jnp.asarray(take_c4_np)
    take_c0 = jnp.asarray(take_c0_np)
    weight = penalty.reshape(VARS, 1, 1)
    mesh_size = lax.axis_size("mesh")
    sect_size = lax.axis_size("sect")
    devices = mesh_size * sect_size
    my_mesh = lax.axis_index("mesh")
    my_sect = lax.axis_index("sect")

    forward = [(i, (i + 1) % mesh_size) for i in range(mesh_size)]
    backward = [(j, i) for i, j in forward]
    west_send = jnp.einsum(
        "nm,vme->vne", west_sel, fields[:, :, elements - 1 :], precision=highest_value
    )
    east_send = jnp.einsum("nm,vme->vne", east_sel, fields[:, :, :1], precision=highest_value)
    west_halo = lax.ppermute(west_send, "mesh", forward)
    east_halo = lax.ppermute(east_send, "mesh", backward)
    upward = [(i, i + 1) for i in range(sect_size - 1)]
    downward = [(j, i) for i, j in upward]
    top_rows = fields[:, 4::5]
    bottom_rows = fields[:, 0::5]
    from_below = lax.ppermute(top_rows, "sect", upward)
    from_above = lax.ppermute(bottom_rows, "sect", downward)

    selector = (face_element[:, None] == jnp.arange(elements, dtype=jnp.int32)[None, :]).astype(
        jnp.float32
    )
    rotor_rows = jnp.einsum("vqe,fe->vqf", fields[:, 0:25], selector, precision=highest_value)
    stator = jnp.einsum("vqe,fe->vqf", fields[:, 100:125], selector, precision=highest_value)

    combined = jnp.einsum(
        "dso,dnm->snom", flux_jacobian, volume_operator, precision=highest_value
    )
    volume = jnp.einsum("snom,ome->sne", combined, fields, precision=highest_value)

    west_part = jnp.einsum("nm,vme->vne", west_sel, fields, precision=highest_value)
    east_part = jnp.einsum("nm,vme->vne", east_sel, fields, precision=highest_value)
    west_beyond = jnp.concatenate([west_halo, west_part[:, :, : elements - 1]], axis=2)
    east_beyond = jnp.concatenate([east_part[:, :, 1:], east_halo], axis=2)
    lower_beyond = jnp.einsum("jn,vje->vne", take_c0, from_below, precision=highest_value)
    upper_beyond = jnp.einsum("jn,vje->vne", take_c4, from_above, precision=highest_value)
    stator_lift = jnp.einsum("vqf,fe->vqe", weight * stator, selector, precision=highest_value)
    stator_full = jnp.concatenate(
        [jnp.zeros((VARS, 100, elements), jnp.float32), stator_lift], axis=1
    )
    neighbours = west_beyond + east_beyond + lower_beyond + upper_beyond
    base_tendency = volume + weight * (neighbours - jnp.asarray(count_np) * fields) - stator_full

    top_base = fields[VARS - 1, 100:125] + segment_gain * (
        segment_decay * segment_register[VARS - 1, 100:125]
        + time_step * base_tendency[VARS - 1, 100:125]
    )
    sampled = jnp.einsum("qe,fe->qf", top_base, selector, precision=highest_value)
    surface_base = jnp.mean(sampled, axis=0)
    rotor_sum = jnp.sum(rotor_rows[VARS - 1], axis=0)

    shift = rotation[0] // face_count
    within = rotation[0] % face_count
    slots = jnp.arange(face_count, dtype=jnp.int32)
    dest_mesh = jnp.arange(mesh_size, dtype=jnp.int32)
    first = dest_mesh == (my_mesh - shift) % mesh_size
    second = dest_mesh == (my_mesh - shift - 1) % mesh_size
    keep = (first[:, None] & (slots >= within)[None, :]) | (
        second[:, None] & (slots < within)[None, :]
    )
    rotor_send = jnp.where(keep[:, None, None, :], rotor_rows[None], 0.0).reshape(mesh_size, -1)
    shared = jnp.concatenate(
        [
            pressure_history.astype(jnp.float32).reshape(-1),
            surface_geometry.astype(jnp.float32).reshape(-1),
            face_element.astype(jnp.float32),
            surface_base,
            rotor_sum,
            rotation.astype(jnp.float32),
        ]
    )
    shared_sect = lax.all_gather(shared[None], "sect", axis=0, tiled=True).reshape(-1)
    send = jnp.concatenate(
        [rotor_send, jnp.broadcast_to(shared_sect[None], (mesh_size, shared_sect.shape[0]))],
        axis=1,
    )
    recv = lax.all_to_all(send, "mesh", 0, 0, tiled=True)

    rotor_width = VARS * 25 * face_count
    near_slab = (my_mesh + shift) % mesh_size
    far_slab = (near_slab + 1) % mesh_size
    arrived = (
        lax.dynamic_index_in_dim(recv, near_slab, 0, keepdims=False)
        + lax.dynamic_index_in_dim(recv, far_slab, 0, keepdims=False)
    )[:rotor_width].reshape(VARS, 25, face_count)
    order = (slots + within) % face_count
    rotated = jnp.take(arrived, order, axis=2)
    rotor_lift = jnp.einsum("vqf,fe->vqe", weight * rotated, selector, precision=highest_value)
    rotor_full = jnp.concatenate(
        [jnp.zeros((VARS, 100, elements), jnp.float32), rotor_lift], axis=1
    )
    rate_tendency = base_tendency + rotor_full
    new_register = segment_decay * segment_register + time_step * rate_tendency
    new_fields = fields + segment_gain * new_register

    info = recv[:, rotor_width:].reshape(devices, shared.shape[0])
    rows = jnp.transpose(info)
    hist_rows = pressure_history.shape[0]
    geo_at = hist_rows * face_count
    fe_at = geo_at + 6 * face_count
    base_at = fe_at + face_count
    sum_at = base_at + face_count
    rot_at = sum_at + face_count
    all_fe = rows[fe_at : fe_at + face_count]
    all_base = rows[base_at : base_at + face_count]
    all_sum = info[:, sum_at : sum_at + face_count]
    cycle = mesh_size * face_count
    by_sect = jnp.transpose(all_sum.reshape(mesh_size, sect_size, face_count), (1, 0, 2)).reshape(
        sect_size, cycle
    )
    doubled = jnp.concatenate([by_sect, by_sect], axis=1)
    rolled = jnp.stack(
        [
            lax.dynamic_slice_in_dim(doubled[k], info[k, rot_at].astype(jnp.int32) % cycle, cycle)
            for k in range(sect_size)
        ]
    )
    rolled = jnp.transpose(rolled.reshape(sect_size, mesh_size, face_count), (2, 1, 0)).reshape(
        face_count, devices
    )
    same = (all_fe[:, None, :] == all_fe[None, :, :]).astype(jnp.float32)
    rotor_part = jnp.sum(same * rolled[None, :, :], axis=1)
    gain = segment_gain * time_step * penalty[VARS - 1] / 25.0
    surface_now = (all_base + gain * rotor_part).astype(jnp.bfloat16)

    delays = delay_table[:, 0][None, :]
    running = jnp.zeros((TB, observer_sites.shape[1]), jnp.float32)
    for j in range(face_count):
        history = jnp.concatenate(
            [rows[j:geo_at:face_count].astype(jnp.bfloat16), surface_now[j : j + 1]], axis=0
        )
        window = jnp.zeros((TB + 1, devices), jnp.bfloat16)
        for bin_ in range(NB):
            window = jnp.where(
                delays == bin_, history[NB - 1 - bin_ : NB - 1 - bin_ + TB + 1], window
            )
        window_late = window[1:]
        change = (window_late.astype(jnp.float32) - window[:-1].astype(jnp.float32)).astype(
            jnp.bfloat16
        )
        geometry = jnp.stack([info[:, geo_at + i * face_count + j] for i in range(6)])
        near_kernel, rate_kernel = far_kernels(geometry, observer_sites)
        running = running + jnp.dot(
            window_late, near_kernel, preferred_element_type=jnp.float32
        ) + jnp.dot(change, rate_kernel, preferred_element_type=jnp.float32)
    return (new_fields, new_register, running)


def solution(mesh):
    placed = (
        P(None, None, ALL),
        P(None, None, ALL),
        P(),
        P(),
        P(),
        P(ALL),
        P("sect"),
        P(None, ALL),
        P(None, ALL),
        P(None, ALL),
        P(None, ALL),
    )
    return jax.shard_map(
        per_device,
        mesh=mesh,
        in_specs=placed,
        out_specs=(
            P(None, None, ALL),
            P(None, None, ALL),
            P(None, ALL),
        ),
        check_vma=False,
    )
```

```python
import numpy as np
import jax
import jax.numpy as jnp
from jax import lax
from jax.sharding import PartitionSpec as P

VARS = 5
NODES = 125
FACE_DEV = 4
TB = 8
NB = 8

segment_decay = -0.4178904745
segment_gain = 1.4061
time_step = 0.2
four_pi = 12.566370614359172
highest_value = lax.Precision.HIGHEST
ALL = ("mesh", "sect")


def node_tables():
    a, b, c = np.meshgrid(np.arange(5), np.arange(5), np.arange(5), indexing="ij")
    a, b, c = a.reshape(-1), b.reshape(-1), c.reshape(-1)
    n = np.arange(NODES)
    west = np.zeros((NODES, NODES), np.float32)
    west[n[b == 0], n[b == 0] + 20] = 1.0
    east = np.zeros((NODES, NODES), np.float32)
    east[n[b == 4], n[b == 4] - 20] = 1.0
    take_c4 = np.zeros((25, NODES), np.float32)
    take_c4[np.arange(25), n[c == 4]] = 1.0
    take_c0 = np.zeros((25, NODES), np.float32)
    take_c0[np.arange(25), n[c == 0]] = 1.0
    count = ((b == 0).astype(np.float32) + (b == 4) + (c == 0) + (c == 4)).reshape(1, NODES, 1)
    return west, east, take_c4, take_c0, count


def flat_gather(value, axes):
    size = value.size
    whole = lax.all_gather(value.reshape(size), axes, axis=0, tiled=True)
    return whole.reshape((-1,) + value.shape)


def far_kernels(geometry, observers):
    separation = observers[:, None, :] - geometry[:3, :, None]
    square = jnp.sum(separation * separation, axis=0)
    radius = jnp.sqrt(square)
    normal_part = jnp.sum(geometry[3:6, :, None] * separation, axis=0)
    near_kernel = (normal_part / (four_pi * square * radius)).astype(jnp.bfloat16)
    rate_kernel = (normal_part / (four_pi * square)).astype(jnp.bfloat16)
    return (near_kernel, rate_kernel)


def per_device(
    fields,
    segment_register,
    volume_operator,
    flux_jacobian,
    penalty,
    face_element,
    rotation,
    pressure_history,
    surface_geometry,
    observer_sites,
    delay_table,
):
    elements = fields.shape[2]
    face_count = face_element.shape[0]
    west_np, east_np, take_c4_np, take_c0_np, count_np = node_tables()
    west_sel = jnp.asarray(west_np)
    east_sel = jnp.asarray(east_np)
    take_c4 = jnp.asarray(take_c4_np)
    take_c0 = jnp.asarray(take_c0_np)
    weight = penalty.reshape(VARS, 1, 1)
    mesh_size = lax.axis_size("mesh")
    sect_size = lax.axis_size("sect")
    devices = mesh_size * sect_size
    my_mesh = lax.axis_index("mesh")
    my_sect = lax.axis_index("sect")

    forward = [(i, (i + 1) % mesh_size) for i in range(mesh_size)]
    backward = [(j, i) for i, j in forward]
    west_send = jnp.einsum(
        "nm,vme->vne", west_sel, fields[:, :, elements - 1 :], precision=highest_value
    )
    east_send = jnp.einsum("nm,vme->vne", east_sel, fields[:, :, :1], precision=highest_value)
    west_halo = lax.ppermute(west_send, "mesh", forward)
    east_halo = lax.ppermute(east_send, "mesh", backward)
    upward = [(i, i + 1) for i in range(sect_size - 1)]
    downward = [(j, i) for i, j in upward]
    top_rows = fields[:, 4::5]
    bottom_rows = fields[:, 0::5]
    from_below = lax.ppermute(top_rows, "sect", upward)
    from_above = lax.ppermute(bottom_rows, "sect", downward)

    selector = (face_element[:, None] == jnp.arange(elements, dtype=jnp.int32)[None, :]).astype(
        jnp.float32
    )
    rotor_rows = jnp.einsum("vqe,fe->vqf", fields[:, 0:25], selector, precision=highest_value)
    stator = jnp.einsum("vqe,fe->vqf", fields[:, 100:125], selector, precision=highest_value)

    combined = jnp.einsum(
        "dso,dnm->snom", flux_jacobian, volume_operator, precision=highest_value
    )
    volume = jnp.einsum("snom,ome->sne", combined, fields, precision=highest_value)

    west_part = jnp.einsum("nm,vme->vne", west_sel, fields, precision=highest_value)
    east_part = jnp.einsum("nm,vme->vne", east_sel, fields, precision=highest_value)
    west_beyond = jnp.concatenate([west_halo, west_part[:, :, : elements - 1]], axis=2)
    east_beyond = jnp.concatenate([east_part[:, :, 1:], east_halo], axis=2)
    lower_beyond = jnp.einsum("jn,vje->vne", take_c0, from_below, precision=highest_value)
    upper_beyond = jnp.einsum("jn,vje->vne", take_c4, from_above, precision=highest_value)
    stator_lift = jnp.einsum("vqf,fe->vqe", weight * stator, selector, precision=highest_value)
    stator_full = jnp.concatenate(
        [jnp.zeros((VARS, 100, elements), jnp.float32), stator_lift], axis=1
    )
    neighbours = west_beyond + east_beyond + lower_beyond + upper_beyond
    base_tendency = volume + weight * (neighbours - jnp.asarray(count_np) * fields) - stator_full

    top_base = fields[VARS - 1, 100:125] + segment_gain * (
        segment_decay * segment_register[VARS - 1, 100:125]
        + time_step * base_tendency[VARS - 1, 100:125]
    )
    sampled = jnp.einsum("qe,fe->qf", top_base, selector, precision=highest_value)
    surface_base = jnp.mean(sampled, axis=0)
    rotor_sum = jnp.sum(rotor_rows[VARS - 1], axis=0)

    shift = rotation[0] // face_count
    within = rotation[0] % face_count
    slots = jnp.arange(face_count, dtype=jnp.int32)
    dest_mesh = jnp.arange(mesh_size, dtype=jnp.int32)
    first = dest_mesh == (my_mesh - shift) % mesh_size
    second = dest_mesh == (my_mesh - shift - 1) % mesh_size
    keep = (first[:, None] & (slots >= within)[None, :]) | (
        second[:, None] & (slots < within)[None, :]
    )
    rotor_send = jnp.where(keep[:, None, None, :], rotor_rows[None], 0.0).reshape(mesh_size, -1)
    rotor_send = rotor_send.astype(jnp.bfloat16)
    exact = jnp.concatenate([surface_base, rotor_sum])
    exact_hi = exact.astype(jnp.bfloat16)
    exact_rest = exact - exact_hi.astype(jnp.float32)
    exact_mid = exact_rest.astype(jnp.bfloat16)
    exact_lo = (exact_rest - exact_mid.astype(jnp.float32)).astype(jnp.bfloat16)
    turn = rotation.astype(jnp.float32)
    turn_hi = turn.astype(jnp.bfloat16)
    turn_lo = (turn - turn_hi.astype(jnp.float32)).astype(jnp.bfloat16)
    shared = jnp.concatenate(
        [
            pressure_history.reshape(-1),
            surface_geometry.reshape(-1),
            face_element.astype(jnp.bfloat16),
            exact_hi,
            exact_mid,
            exact_lo,
            turn_hi,
            turn_lo,
        ]
    )
    shared_sect = lax.all_gather(shared[None], "sect", axis=0, tiled=True).reshape(-1)
    send = jnp.concatenate(
        [rotor_send, jnp.broadcast_to(shared_sect[None], (mesh_size, shared_sect.shape[0]))],
        axis=1,
    )
    recv = lax.all_to_all(send, "mesh", 0, 0, tiled=True)

    rotor_width = VARS * 25 * face_count
    near_slab = (my_mesh + shift) % mesh_size
    far_slab = (near_slab + 1) % mesh_size
    arrived = (
        lax.dynamic_index_in_dim(recv, near_slab, 0, keepdims=False)
        + lax.dynamic_index_in_dim(recv, far_slab, 0, keepdims=False)
    )[:rotor_width].astype(jnp.float32).reshape(VARS, 25, face_count)
    order = (slots + within) % face_count
    rotated = jnp.take(arrived, order, axis=2)
    rotor_lift = jnp.einsum("vqf,fe->vqe", weight * rotated, selector, precision=highest_value)
    rotor_full = jnp.concatenate(
        [jnp.zeros((VARS, 100, elements), jnp.float32), rotor_lift], axis=1
    )
    rate_tendency = base_tendency + rotor_full
    new_register = segment_decay * segment_register + time_step * rate_tendency
    new_fields = fields + segment_gain * new_register

    info = recv[:, rotor_width:].reshape(devices, shared.shape[0]).astype(jnp.float32)
    hist_rows = pressure_history.shape[0]
    geo_at = hist_rows * face_count
    fe_at = geo_at + 6 * face_count
    hi_at = fe_at + face_count
    mid_at = hi_at + 2 * face_count
    lo_at = mid_at + 2 * face_count
    turn_at = lo_at + 2 * face_count
    exact_all = (
        info[:, hi_at : hi_at + 2 * face_count] + info[:, mid_at : mid_at + 2 * face_count]
    ) + info[:, lo_at : lo_at + 2 * face_count]
    turn_all = info[:, turn_at] + info[:, turn_at + 1]
    rows = jnp.transpose(info)
    base_rows = jnp.transpose(exact_all[:, :face_count])
    all_fe = rows[fe_at : fe_at + face_count]
    all_base = base_rows
    all_sum = exact_all[:, face_count:]
    cycle = mesh_size * face_count
    by_sect = jnp.transpose(all_sum.reshape(mesh_size, sect_size, face_count), (1, 0, 2)).reshape(
        sect_size, cycle
    )
    doubled = jnp.concatenate([by_sect, by_sect], axis=1)
    rolled = jnp.stack(
        [
            lax.dynamic_slice_in_dim(doubled[k], turn_all[k].astype(jnp.int32) % cycle, cycle)
            for k in range(sect_size)
        ]
    )
    rolled = jnp.transpose(rolled.reshape(sect_size, mesh_size, face_count), (2, 1, 0)).reshape(
        face_count, devices
    )
    same = (all_fe[:, None, :] == all_fe[None, :, :]).astype(jnp.float32)
    rotor_part = jnp.sum(same * rolled[None, :, :], axis=1)
    gain = segment_gain * time_step * penalty[VARS - 1] / 25.0
    surface_now = (all_base + gain * rotor_part).astype(jnp.bfloat16)

    delays = delay_table[:, 0][None, :]
    running = jnp.zeros((TB, observer_sites.shape[1]), jnp.float32)
    for j in range(face_count):
        history = jnp.concatenate(
            [rows[j:geo_at:face_count].astype(jnp.bfloat16), surface_now[j : j + 1]], axis=0
        )
        window = jnp.zeros((TB + 1, devices), jnp.bfloat16)
        for bin_ in range(NB):
            window = jnp.where(
                delays == bin_, history[NB - 1 - bin_ : NB - 1 - bin_ + TB + 1], window
            )
        window_late = window[1:]
        change = (window_late.astype(jnp.float32) - window[:-1].astype(jnp.float32)).astype(
            jnp.bfloat16
        )
        geometry = jnp.stack([info[:, geo_at + i * face_count + j] for i in range(6)])
        near_kernel, rate_kernel = far_kernels(geometry, observer_sites)
        running = running + jnp.dot(
            window_late, near_kernel, preferred_element_type=jnp.float32
        ) + jnp.dot(change, rate_kernel, preferred_element_type=jnp.float32)
    return (new_fields, new_register, running)


def solution(mesh):
    placed = (
        P(None, None, ALL),
        P(None, None, ALL),
        P(),
        P(),
        P(),
        P(ALL),
        P("sect"),
        P(None, ALL),
        P(None, ALL),
        P(None, ALL),
        P(None, ALL),
    )
    return jax.shard_map(
        per_device,
        mesh=mesh,
        in_specs=placed,
        out_specs=(
            P(None, None, ALL),
            P(None, None, ALL),
            P(None, ALL),
        ),
        check_vma=False,
    )
```

```python
import numpy as np
import jax
import jax.numpy as jnp
from jax import lax
from jax.sharding import PartitionSpec as P

VARS = 5
NODES = 125
FACE_DEV = 4
TB = 8
NB = 8

segment_decay = -0.4178904745
segment_gain = 1.4061
time_step = 0.2
four_pi = 12.566370614359172
highest_value = lax.Precision.HIGHEST
ALL = ("mesh", "sect")


def node_tables():
    a, b, c = np.meshgrid(np.arange(5), np.arange(5), np.arange(5), indexing="ij")
    a, b, c = a.reshape(-1), b.reshape(-1), c.reshape(-1)
    n = np.arange(NODES)
    west = np.zeros((NODES, NODES), np.float32)
    west[n[b == 0], n[b == 0] + 20] = 1.0
    east = np.zeros((NODES, NODES), np.float32)
    east[n[b == 4], n[b == 4] - 20] = 1.0
    take_c4 = np.zeros((25, NODES), np.float32)
    take_c4[np.arange(25), n[c == 4]] = 1.0
    take_c0 = np.zeros((25, NODES), np.float32)
    take_c0[np.arange(25), n[c == 0]] = 1.0
    count = ((b == 0).astype(np.float32) + (b == 4) + (c == 0) + (c == 4)).reshape(1, NODES, 1)
    return west, east, take_c4, take_c0, count


def flat_gather(value, axes):
    size = value.size
    whole = lax.all_gather(value.reshape(size), axes, axis=0, tiled=True)
    return whole.reshape((-1,) + value.shape)


def far_kernels(geometry, observers):
    separation = observers[:, None, :] - geometry[:3, :, None]
    square = jnp.sum(separation * separation, axis=0)
    radius = jnp.sqrt(square)
    normal_part = jnp.sum(geometry[3:6, :, None] * separation, axis=0)
    near_kernel = (normal_part / (four_pi * square * radius)).astype(jnp.bfloat16)
    rate_kernel = (normal_part / (four_pi * square)).astype(jnp.bfloat16)
    return (near_kernel, rate_kernel)


def far_kernels_by_observer(geometry, observers):
    separation = observers[:, :, None] - geometry[:3, None, :]
    square = jnp.sum(separation * separation, axis=0)
    radius = jnp.sqrt(square)
    normal_part = jnp.sum(geometry[3:6, None, :] * separation, axis=0)
    near_kernel = (normal_part / (four_pi * square * radius)).astype(jnp.bfloat16)
    rate_kernel = (normal_part / (four_pi * square)).astype(jnp.bfloat16)
    return (near_kernel, rate_kernel)


def per_device(
    fields,
    segment_register,
    volume_operator,
    flux_jacobian,
    penalty,
    face_element,
    rotation,
    pressure_history,
    surface_geometry,
    observer_sites,
    delay_table,
):
    elements = fields.shape[2]
    face_count = face_element.shape[0]
    west_np, east_np, take_c4_np, take_c0_np, count_np = node_tables()
    west_sel = jnp.asarray(west_np)
    east_sel = jnp.asarray(east_np)
    take_c4 = jnp.asarray(take_c4_np)
    take_c0 = jnp.asarray(take_c0_np)
    weight = penalty.reshape(VARS, 1, 1)
    mesh_size = lax.axis_size("mesh")
    sect_size = lax.axis_size("sect")
    devices = mesh_size * sect_size
    my_mesh = lax.axis_index("mesh")
    my_sect = lax.axis_index("sect")

    forward = [(i, (i + 1) % mesh_size) for i in range(mesh_size)]
    backward = [(j, i) for i, j in forward]
    west_send = jnp.einsum(
        "nm,vme->vne", west_sel, fields[:, :, elements - 1 :], precision=highest_value
    )
    east_send = jnp.einsum("nm,vme->vne", east_sel, fields[:, :, :1], precision=highest_value)
    west_halo = lax.ppermute(west_send, "mesh", forward)
    east_halo = lax.ppermute(east_send, "mesh", backward)
    upward = [(i, i + 1) for i in range(sect_size - 1)]
    downward = [(j, i) for i, j in upward]
    top_rows = fields[:, 4::5]
    bottom_rows = fields[:, 0::5]
    from_below = lax.ppermute(top_rows, "sect", upward)
    from_above = lax.ppermute(bottom_rows, "sect", downward)

    selector = (face_element[:, None] == jnp.arange(elements, dtype=jnp.int32)[None, :]).astype(
        jnp.float32
    )
    rotor_rows = jnp.einsum("vqe,fe->vqf", fields[:, 0:25], selector, precision=highest_value)
    stator = jnp.einsum("vqe,fe->vqf", fields[:, 100:125], selector, precision=highest_value)

    combined = jnp.einsum(
        "dso,dnm->snom", flux_jacobian, volume_operator, precision=highest_value
    )
    volume = jnp.einsum("snom,ome->sne", combined, fields, precision=highest_value)

    west_part = jnp.einsum("nm,vme->vne", west_sel, fields, precision=highest_value)
    east_part = jnp.einsum("nm,vme->vne", east_sel, fields, precision=highest_value)
    west_beyond = jnp.concatenate([west_halo, west_part[:, :, : elements - 1]], axis=2)
    east_beyond = jnp.concatenate([east_part[:, :, 1:], east_halo], axis=2)
    lower_beyond = jnp.einsum("jn,vje->vne", take_c0, from_below, precision=highest_value)
    upper_beyond = jnp.einsum("jn,vje->vne", take_c4, from_above, precision=highest_value)
    stator_lift = jnp.einsum("vqf,fe->vqe", weight * stator, selector, precision=highest_value)
    stator_full = jnp.concatenate(
        [jnp.zeros((VARS, 100, elements), jnp.float32), stator_lift], axis=1
    )
    neighbours = west_beyond + east_beyond + lower_beyond + upper_beyond
    base_tendency = volume + weight * (neighbours - jnp.asarray(count_np) * fields) - stator_full

    top_base = fields[VARS - 1, 100:125] + segment_gain * (
        segment_decay * segment_register[VARS - 1, 100:125]
        + time_step * base_tendency[VARS - 1, 100:125]
    )
    sampled = jnp.einsum("qe,fe->qf", top_base, selector, precision=highest_value)
    surface_base = jnp.mean(sampled, axis=0)
    rotor_sum = jnp.sum(rotor_rows[VARS - 1], axis=0)

    shift = rotation[0] // face_count
    within = rotation[0] % face_count
    slots = jnp.arange(face_count, dtype=jnp.int32)
    dest_mesh = jnp.arange(mesh_size, dtype=jnp.int32)
    first = dest_mesh == (my_mesh - shift) % mesh_size
    second = dest_mesh == (my_mesh - shift - 1) % mesh_size
    keep = (first[:, None] & (slots >= within)[None, :]) | (
        second[:, None] & (slots < within)[None, :]
    )
    rotor_send = jnp.where(keep[:, None, None, :], rotor_rows[None], 0.0).reshape(mesh_size, -1)
    rotor_send = rotor_send.astype(jnp.bfloat16)
    exact = jnp.concatenate([surface_base, rotor_sum])
    exact_hi = exact.astype(jnp.bfloat16)
    exact_rest = exact - exact_hi.astype(jnp.float32)
    exact_mid = exact_rest.astype(jnp.bfloat16)
    exact_lo = (exact_rest - exact_mid.astype(jnp.float32)).astype(jnp.bfloat16)
    turn = rotation.astype(jnp.float32)
    turn_hi = turn.astype(jnp.bfloat16)
    turn_lo = (turn - turn_hi.astype(jnp.float32)).astype(jnp.bfloat16)
    shared = jnp.concatenate(
        [
            pressure_history.reshape(-1),
            surface_geometry.reshape(-1),
            face_element.astype(jnp.bfloat16),
            exact_hi,
            exact_mid,
            exact_lo,
            turn_hi,
            turn_lo,
        ]
    )
    shared_sect = lax.all_gather(shared[None], "sect", axis=0, tiled=True).reshape(-1)
    send = jnp.concatenate(
        [rotor_send, jnp.broadcast_to(shared_sect[None], (mesh_size, shared_sect.shape[0]))],
        axis=1,
    )
    recv = lax.all_to_all(send, "mesh", 0, 0, tiled=True)

    rotor_width = VARS * 25 * face_count
    near_slab = (my_mesh + shift) % mesh_size
    far_slab = (near_slab + 1) % mesh_size
    arrived = (
        lax.dynamic_index_in_dim(recv, near_slab, 0, keepdims=False)
        + lax.dynamic_index_in_dim(recv, far_slab, 0, keepdims=False)
    )[:rotor_width].astype(jnp.float32).reshape(VARS, 25, face_count)
    order = (slots + within) % face_count
    rotated = jnp.take(arrived, order, axis=2)
    rotor_lift = jnp.einsum("vqf,fe->vqe", weight * rotated, selector, precision=highest_value)
    rotor_full = jnp.concatenate(
        [jnp.zeros((VARS, 100, elements), jnp.float32), rotor_lift], axis=1
    )
    rate_tendency = base_tendency + rotor_full
    new_register = segment_decay * segment_register + time_step * rate_tendency
    new_fields = fields + segment_gain * new_register

    info = recv[:, rotor_width:].reshape(devices, shared.shape[0]).astype(jnp.float32)
    hist_rows = pressure_history.shape[0]
    geo_at = hist_rows * face_count
    fe_at = geo_at + 6 * face_count
    hi_at = fe_at + face_count
    mid_at = hi_at + 2 * face_count
    lo_at = mid_at + 2 * face_count
    turn_at = lo_at + 2 * face_count
    exact_all = (
        info[:, hi_at : hi_at + 2 * face_count] + info[:, mid_at : mid_at + 2 * face_count]
    ) + info[:, lo_at : lo_at + 2 * face_count]
    turn_all = info[:, turn_at] + info[:, turn_at + 1]
    rows = jnp.transpose(info)
    base_rows = jnp.transpose(exact_all[:, :face_count])
    all_fe = rows[fe_at : fe_at + face_count]
    all_base = base_rows
    all_sum = exact_all[:, face_count:]
    cycle = mesh_size * face_count
    by_sect = jnp.transpose(all_sum.reshape(mesh_size, sect_size, face_count), (1, 0, 2)).reshape(
        sect_size, cycle
    )
    doubled = jnp.concatenate([by_sect, by_sect], axis=1)
    rolled = jnp.stack(
        [
            lax.dynamic_slice_in_dim(doubled[k], turn_all[k].astype(jnp.int32) % cycle, cycle)
            for k in range(sect_size)
        ]
    )
    rolled = jnp.transpose(rolled.reshape(sect_size, mesh_size, face_count), (2, 1, 0)).reshape(
        face_count, devices
    )
    same = (all_fe[:, None, :] == all_fe[None, :, :]).astype(jnp.float32)
    rotor_part = jnp.sum(same * rolled[None, :, :], axis=1)
    gain = segment_gain * time_step * penalty[VARS - 1] / 25.0
    surface_now = (all_base + gain * rotor_part).astype(jnp.bfloat16)

    delays = delay_table[:, 0][None, :]
    running = jnp.zeros((TB, observer_sites.shape[1]), jnp.float32)
    for j in range(face_count):
        history = jnp.concatenate(
            [rows[j:geo_at:face_count].astype(jnp.bfloat16), surface_now[j : j + 1]], axis=0
        )
        window = jnp.zeros((TB + 1, devices), jnp.bfloat16)
        for bin_ in range(NB):
            window = jnp.where(
                delays == bin_, history[NB - 1 - bin_ : NB - 1 - bin_ + TB + 1], window
            )
        window_late = window[1:]
        change = (window_late.astype(jnp.float32) - window[:-1].astype(jnp.float32)).astype(
            jnp.bfloat16
        )
        geometry = rows[geo_at + j : fe_at : face_count]
        near_kernel, rate_kernel = far_kernels_by_observer(geometry, observer_sites)
        contract = (((1,), (1,)), ((), ()))
        running = running + lax.dot_general(
            window_late, near_kernel, contract, preferred_element_type=jnp.float32
        ) + lax.dot_general(change, rate_kernel, contract, preferred_element_type=jnp.float32)
    return (new_fields, new_register, running)


def solution(mesh):
    placed = (
        P(None, None, ALL),
        P(None, None, ALL),
        P(),
        P(),
        P(),
        P(ALL),
        P("sect"),
        P(None, ALL),
        P(None, ALL),
        P(None, ALL),
        P(None, ALL),
    )
    return jax.shard_map(
        per_device,
        mesh=mesh,
        in_specs=placed,
        out_specs=(
            P(None, None, ALL),
            P(None, None, ALL),
            P(None, ALL),
        ),
        check_vma=False,
    )
```

```python
import numpy as np
import jax
import jax.numpy as jnp
from jax import lax
from jax.sharding import PartitionSpec as P

VARS = 5
NODES = 125
FACE_DEV = 4
TB = 8
NB = 8

segment_decay = -0.4178904745
segment_gain = 1.4061
time_step = 0.2
four_pi = 12.566370614359172
highest_value = lax.Precision.HIGHEST
ALL = ("mesh", "sect")


def node_tables():
    a, b, c = np.meshgrid(np.arange(5), np.arange(5), np.arange(5), indexing="ij")
    a, b, c = a.reshape(-1), b.reshape(-1), c.reshape(-1)
    n = np.arange(NODES)
    west = np.zeros((NODES, NODES), np.float32)
    west[n[b == 0], n[b == 0] + 20] = 1.0
    east = np.zeros((NODES, NODES), np.float32)
    east[n[b == 4], n[b == 4] - 20] = 1.0
    take_c4 = np.zeros((25, NODES), np.float32)
    take_c4[np.arange(25), n[c == 4]] = 1.0
    take_c0 = np.zeros((25, NODES), np.float32)
    take_c0[np.arange(25), n[c == 0]] = 1.0
    count = ((b == 0).astype(np.float32) + (b == 4) + (c == 0) + (c == 4)).reshape(1, NODES, 1)
    take_b4 = np.zeros((25, NODES), np.float32)
    take_b4[np.arange(25), n[b == 4]] = 1.0
    take_b0 = np.zeros((25, NODES), np.float32)
    take_b0[np.arange(25), n[b == 0]] = 1.0
    return west, east, take_c4, take_c0, count, take_b4, take_b0


def flat_gather(value, axes):
    size = value.size
    whole = lax.all_gather(value.reshape(size), axes, axis=0, tiled=True)
    return whole.reshape((-1,) + value.shape)


def far_kernels(geometry, observers):
    separation = observers[:, None, :] - geometry[:3, :, None]
    square = jnp.sum(separation * separation, axis=0)
    radius = jnp.sqrt(square)
    normal_part = jnp.sum(geometry[3:6, :, None] * separation, axis=0)
    near_kernel = (normal_part / (four_pi * square * radius)).astype(jnp.bfloat16)
    rate_kernel = (normal_part / (four_pi * square)).astype(jnp.bfloat16)
    return (near_kernel, rate_kernel)


def far_kernels_by_observer(geometry, observers):
    separation = observers[:, :, None] - geometry[:3, None, :]
    square = jnp.sum(separation * separation, axis=0)
    radius = jnp.sqrt(square)
    normal_part = jnp.sum(geometry[3:6, None, :] * separation, axis=0)
    near_kernel = (normal_part / (four_pi * square * radius)).astype(jnp.bfloat16)
    rate_kernel = (normal_part / (four_pi * square)).astype(jnp.bfloat16)
    return (near_kernel, rate_kernel)


def per_device(
    fields,
    segment_register,
    volume_operator,
    flux_jacobian,
    penalty,
    face_element,
    rotation,
    pressure_history,
    surface_geometry,
    observer_sites,
    delay_table,
):
    elements = fields.shape[2]
    face_count = face_element.shape[0]
    west_np, east_np, take_c4_np, take_c0_np, count_np, take_b4_np, take_b0_np = node_tables()
    take_b4 = jnp.asarray(take_b4_np)
    take_b0 = jnp.asarray(take_b0_np)
    west_sel = jnp.asarray(west_np)
    east_sel = jnp.asarray(east_np)
    take_c4 = jnp.asarray(take_c4_np)
    take_c0 = jnp.asarray(take_c0_np)
    weight = penalty.reshape(VARS, 1, 1)
    mesh_size = lax.axis_size("mesh")
    sect_size = lax.axis_size("sect")
    devices = mesh_size * sect_size
    my_mesh = lax.axis_index("mesh")
    my_sect = lax.axis_index("sect")

    west_send = jnp.einsum(
        "jm,vm->vj", take_b4, fields[:, :, elements - 1], precision=highest_value
    )
    east_send = jnp.einsum("jm,vm->vj", take_b0, fields[:, :, 0], precision=highest_value)
    upward = [(i, i + 1) for i in range(sect_size - 1)]
    downward = [(j, i) for i, j in upward]
    top_rows = fields[:, 4::5]
    bottom_rows = fields[:, 0::5]
    from_below = lax.ppermute(top_rows, "sect", upward)
    from_above = lax.ppermute(bottom_rows, "sect", downward)

    selector = (face_element[:, None] == jnp.arange(elements, dtype=jnp.int32)[None, :]).astype(
        jnp.float32
    )
    rotor_rows = jnp.einsum("vqe,fe->vqf", fields[:, 0:25], selector, precision=highest_value)
    stator = jnp.einsum("vqe,fe->vqf", fields[:, 100:125], selector, precision=highest_value)

    combined = jnp.einsum(
        "dso,dnm->snom", flux_jacobian, volume_operator, precision=highest_value
    )
    volume = jnp.einsum("snom,ome->sne", combined, fields, precision=highest_value)

    west_part = jnp.einsum("nm,vme->vne", west_sel, fields, precision=highest_value)
    east_part = jnp.einsum("nm,vme->vne", east_sel, fields, precision=highest_value)
    edge = jnp.zeros((VARS, NODES, 1), jnp.float32)
    west_beyond = jnp.concatenate([edge, west_part[:, :, : elements - 1]], axis=2)
    east_beyond = jnp.concatenate([east_part[:, :, 1:], edge], axis=2)
    lower_beyond = jnp.einsum("jn,vje->vne", take_c0, from_below, precision=highest_value)
    upper_beyond = jnp.einsum("jn,vje->vne", take_c4, from_above, precision=highest_value)
    stator_lift = jnp.einsum("vqf,fe->vqe", weight * stator, selector, precision=highest_value)
    stator_full = jnp.concatenate(
        [jnp.zeros((VARS, 100, elements), jnp.float32), stator_lift], axis=1
    )
    neighbours = west_beyond + east_beyond + lower_beyond + upper_beyond
    base_tendency = volume + weight * (neighbours - jnp.asarray(count_np) * fields) - stator_full

    top_base = fields[VARS - 1, 100:125] + segment_gain * (
        segment_decay * segment_register[VARS - 1, 100:125]
        + time_step * base_tendency[VARS - 1, 100:125]
    )
    sampled = jnp.einsum("qe,fe->qf", top_base, selector, precision=highest_value)
    surface_base = jnp.mean(sampled, axis=0)
    rotor_sum = jnp.sum(rotor_rows[VARS - 1], axis=0)

    shift = rotation[0] // face_count
    within = rotation[0] % face_count
    slots = jnp.arange(face_count, dtype=jnp.int32)
    dest_mesh = jnp.arange(mesh_size, dtype=jnp.int32)
    first = dest_mesh == (my_mesh - shift) % mesh_size
    second = dest_mesh == (my_mesh - shift - 1) % mesh_size
    keep = (first[:, None] & (slots >= within)[None, :]) | (
        second[:, None] & (slots < within)[None, :]
    )
    rotor_send = jnp.where(keep[:, None, None, :], rotor_rows[None], 0.0).reshape(mesh_size, -1)
    to_next = (dest_mesh == (my_mesh + 1) % mesh_size)[:, None]
    to_prev = (dest_mesh == (my_mesh - 1) % mesh_size)[:, None]
    halo_send = jnp.concatenate(
        [
            jnp.where(to_next, west_send.reshape(1, -1), 0.0),
            jnp.where(to_prev, east_send.reshape(1, -1), 0.0),
        ],
        axis=1,
    )
    rotor_send = jnp.concatenate([rotor_send, halo_send], axis=1).astype(jnp.bfloat16)
    edge_sums = jnp.stack(
        [jnp.sum(west_send[VARS - 1, 20:25]), jnp.sum(east_send[VARS - 1, 20:25])]
    )
    exact = jnp.concatenate([surface_base, rotor_sum, edge_sums])
    exact_hi = exact.astype(jnp.bfloat16)
    exact_rest = exact - exact_hi.astype(jnp.float32)
    exact_mid = exact_rest.astype(jnp.bfloat16)
    exact_lo = (exact_rest - exact_mid.astype(jnp.float32)).astype(jnp.bfloat16)
    turn = rotation.astype(jnp.float32)
    turn_hi = turn.astype(jnp.bfloat16)
    turn_lo = (turn - turn_hi.astype(jnp.float32)).astype(jnp.bfloat16)
    shared = jnp.concatenate(
        [
            pressure_history.reshape(-1),
            surface_geometry.reshape(-1),
            face_element.astype(jnp.bfloat16),
            exact_hi,
            exact_mid,
            exact_lo,
            turn_hi,
            turn_lo,
        ]
    )
    shared_sect = lax.all_gather(shared[None], "sect", axis=0, tiled=True).reshape(-1)
    send = jnp.concatenate(
        [rotor_send, jnp.broadcast_to(shared_sect[None], (mesh_size, shared_sect.shape[0]))],
        axis=1,
    )
    recv = lax.all_to_all(send, "mesh", 0, 0, tiled=True)

    rotor_width = VARS * 25 * face_count
    halo_width = VARS * 25
    prev_slab = (my_mesh - 1) % mesh_size
    next_slab = (my_mesh + 1) % mesh_size
    west_halo = lax.dynamic_index_in_dim(recv, prev_slab, 0, keepdims=False)[
        rotor_width : rotor_width + halo_width
    ].astype(jnp.float32).reshape(VARS, 25)
    east_halo = lax.dynamic_index_in_dim(recv, next_slab, 0, keepdims=False)[
        rotor_width + halo_width : rotor_width + 2 * halo_width
    ].astype(jnp.float32).reshape(VARS, 25)
    west_col = jnp.einsum("jn,vj->vn", take_b0, west_halo, precision=highest_value)
    east_col = jnp.einsum("jn,vj->vn", take_b4, east_halo, precision=highest_value)
    halo_full = jnp.concatenate(
        [
            west_col[:, :, None],
            jnp.zeros((VARS, NODES, elements - 2), jnp.float32),
            east_col[:, :, None],
        ],
        axis=2,
    )
    near_slab = (my_mesh + shift) % mesh_size
    far_slab = (near_slab + 1) % mesh_size
    arrived = (
        lax.dynamic_index_in_dim(recv, near_slab, 0, keepdims=False)
        + lax.dynamic_index_in_dim(recv, far_slab, 0, keepdims=False)
    )[:rotor_width].astype(jnp.float32).reshape(VARS, 25, face_count)
    order = (slots + within) % face_count
    rotated = jnp.take(arrived, order, axis=2)
    rotor_lift = jnp.einsum("vqf,fe->vqe", weight * rotated, selector, precision=highest_value)
    rotor_full = jnp.concatenate(
        [jnp.zeros((VARS, 100, elements), jnp.float32), rotor_lift], axis=1
    )
    rate_tendency = base_tendency + rotor_full + weight * halo_full
    new_register = segment_decay * segment_register + time_step * rate_tendency
    new_fields = fields + segment_gain * new_register

    info = recv[:, rotor_width + 2 * halo_width :].reshape(devices, shared.shape[0])
    info = info.astype(jnp.float32)
    hist_rows = pressure_history.shape[0]
    geo_at = hist_rows * face_count
    fe_at = geo_at + 6 * face_count
    hi_at = fe_at + face_count
    exact_width = 2 * face_count + 2
    mid_at = hi_at + exact_width
    lo_at = mid_at + exact_width
    turn_at = lo_at + exact_width
    exact_all = (
        info[:, hi_at : hi_at + exact_width] + info[:, mid_at : mid_at + exact_width]
    ) + info[:, lo_at : lo_at + exact_width]
    edge_grid = exact_all[:, 2 * face_count :].reshape(mesh_size, sect_size, 2)
    west_sum = jnp.roll(edge_grid[:, :, 0], 1, axis=0).reshape(1, devices)
    east_sum = jnp.roll(edge_grid[:, :, 1], -1, axis=0).reshape(1, devices)
    turn_all = info[:, turn_at] + info[:, turn_at + 1]
    rows = jnp.transpose(info)
    base_rows = jnp.transpose(exact_all[:, :face_count])
    all_fe = rows[fe_at : fe_at + face_count]
    all_base = base_rows
    all_sum = exact_all[:, face_count : 2 * face_count]
    cycle = mesh_size * face_count
    by_sect = jnp.transpose(all_sum.reshape(mesh_size, sect_size, face_count), (1, 0, 2)).reshape(
        sect_size, cycle
    )
    doubled = jnp.concatenate([by_sect, by_sect], axis=1)
    rolled = jnp.stack(
        [
            lax.dynamic_slice_in_dim(doubled[k], turn_all[k].astype(jnp.int32) % cycle, cycle)
            for k in range(sect_size)
        ]
    )
    rolled = jnp.transpose(rolled.reshape(sect_size, mesh_size, face_count), (2, 1, 0)).reshape(
        face_count, devices
    )
    same = (all_fe[:, None, :] == all_fe[None, :, :]).astype(jnp.float32)
    rotor_part = jnp.sum(same * rolled[None, :, :], axis=1)
    gain = segment_gain * time_step * penalty[VARS - 1] / 25.0
    edge_part = jnp.where(all_fe == 0, west_sum, 0.0) + jnp.where(
        all_fe == elements - 1, east_sum, 0.0
    )
    surface_now = (all_base + gain * (rotor_part + edge_part)).astype(jnp.bfloat16)

    delays = delay_table[:, 0][None, :]
    running = jnp.zeros((TB, observer_sites.shape[1]), jnp.float32)
    for j in range(face_count):
        history = jnp.concatenate(
            [rows[j:geo_at:face_count].astype(jnp.bfloat16), surface_now[j : j + 1]], axis=0
        )
        window = jnp.zeros((TB + 1, devices), jnp.bfloat16)
        for bin_ in range(NB):
            window = jnp.where(
                delays == bin_, history[NB - 1 - bin_ : NB - 1 - bin_ + TB + 1], window
            )
        window_late = window[1:]
        change = (window_late.astype(jnp.float32) - window[:-1].astype(jnp.float32)).astype(
            jnp.bfloat16
        )
        geometry = rows[geo_at + j : fe_at : face_count]
        near_kernel, rate_kernel = far_kernels_by_observer(geometry, observer_sites)
        contract = (((1,), (1,)), ((), ()))
        running = running + lax.dot_general(
            window_late, near_kernel, contract, preferred_element_type=jnp.float32
        ) + lax.dot_general(change, rate_kernel, contract, preferred_element_type=jnp.float32)
    return (new_fields, new_register, running)


def solution(mesh):
    placed = (
        P(None, None, ALL),
        P(None, None, ALL),
        P(),
        P(),
        P(),
        P(ALL),
        P("sect"),
        P(None, ALL),
        P(None, ALL),
        P(None, ALL),
        P(None, ALL),
    )
    return jax.shard_map(
        per_device,
        mesh=mesh,
        in_specs=placed,
        out_specs=(
            P(None, None, ALL),
            P(None, None, ALL),
            P(None, ALL),
        ),
        check_vma=False,
    )
```

```python
import numpy as np
import jax
import jax.numpy as jnp
from jax import lax
from jax.sharding import PartitionSpec as P

VARS = 5
NODES = 125
FACE_DEV = 4
TB = 8
NB = 8

segment_decay = -0.4178904745
segment_gain = 1.4061
time_step = 0.2
four_pi = 12.566370614359172
highest_value = lax.Precision.HIGHEST
ALL = ("mesh", "sect")


def node_tables():
    a, b, c = np.meshgrid(np.arange(5), np.arange(5), np.arange(5), indexing="ij")
    a, b, c = a.reshape(-1), b.reshape(-1), c.reshape(-1)
    n = np.arange(NODES)
    west = np.zeros((NODES, NODES), np.float32)
    west[n[b == 0], n[b == 0] + 20] = 1.0
    east = np.zeros((NODES, NODES), np.float32)
    east[n[b == 4], n[b == 4] - 20] = 1.0
    take_c4 = np.zeros((25, NODES), np.float32)
    take_c4[np.arange(25), n[c == 4]] = 1.0
    take_c0 = np.zeros((25, NODES), np.float32)
    take_c0[np.arange(25), n[c == 0]] = 1.0
    count = ((b == 0).astype(np.float32) + (b == 4) + (c == 0) + (c == 4)).reshape(1, NODES, 1)
    return west, east, take_c4, take_c0, count


def flat_gather(value, axes):
    size = value.size
    whole = lax.all_gather(value.reshape(size), axes, axis=0, tiled=True)
    return whole.reshape((-1,) + value.shape)


def far_kernels(geometry, observers):
    separation = observers[:, None, :] - geometry[:3, :, None]
    square = jnp.sum(separation * separation, axis=0)
    radius = jnp.sqrt(square)
    normal_part = jnp.sum(geometry[3:6, :, None] * separation, axis=0)
    near_kernel = (normal_part / (four_pi * square * radius)).astype(jnp.bfloat16)
    rate_kernel = (normal_part / (four_pi * square)).astype(jnp.bfloat16)
    return (near_kernel, rate_kernel)


def far_kernels_by_observer(geometry, observers):
    separation = observers[:, :, None] - geometry[:3, None, :]
    square = jnp.sum(separation * separation, axis=0)
    radius = jnp.sqrt(square)
    normal_part = jnp.sum(geometry[3:6, None, :] * separation, axis=0)
    near_kernel = (normal_part / (four_pi * square * radius)).astype(jnp.bfloat16)
    rate_kernel = (normal_part / (four_pi * square)).astype(jnp.bfloat16)
    return (near_kernel, rate_kernel)


def per_device(
    fields,
    segment_register,
    volume_operator,
    flux_jacobian,
    penalty,
    face_element,
    rotation,
    pressure_history,
    surface_geometry,
    observer_sites,
    delay_table,
):
    elements = fields.shape[2]
    face_count = face_element.shape[0]
    west_np, east_np, take_c4_np, take_c0_np, count_np = node_tables()
    west_sel = jnp.asarray(west_np)
    east_sel = jnp.asarray(east_np)
    take_c4 = jnp.asarray(take_c4_np)
    take_c0 = jnp.asarray(take_c0_np)
    weight = penalty.reshape(VARS, 1, 1)
    mesh_size = lax.axis_size("mesh")
    sect_size = lax.axis_size("sect")
    devices = mesh_size * sect_size
    my_mesh = lax.axis_index("mesh")
    my_sect = lax.axis_index("sect")

    forward = [(i, (i + 1) % mesh_size) for i in range(mesh_size)]
    backward = [(j, i) for i, j in forward]
    west_send = jnp.einsum(
        "nm,vme->vne", west_sel, fields[:, :, elements - 1 :], precision=highest_value
    )
    east_send = jnp.einsum("nm,vme->vne", east_sel, fields[:, :, :1], precision=highest_value)
    west_halo = lax.ppermute(west_send, "mesh", forward)
    east_halo = lax.ppermute(east_send, "mesh", backward)
    upward = [(i, i + 1) for i in range(sect_size - 1)]
    downward = [(j, i) for i, j in upward]
    top_rows = fields[:, 4::5]
    bottom_rows = fields[:, 0::5]
    from_below = lax.ppermute(top_rows.astype(jnp.bfloat16), "sect", upward).astype(jnp.float32)
    from_above = lax.ppermute(bottom_rows.astype(jnp.bfloat16), "sect", downward).astype(
        jnp.float32
    )

    selector = (face_element[:, None] == jnp.arange(elements, dtype=jnp.int32)[None, :]).astype(
        jnp.float32
    )
    rotor_rows = jnp.einsum("vqe,fe->vqf", fields[:, 0:25], selector, precision=highest_value)
    stator = jnp.einsum("vqe,fe->vqf", fields[:, 100:125], selector, precision=highest_value)

    combined = jnp.einsum(
        "dso,dnm->snom", flux_jacobian, volume_operator, precision=highest_value
    )
    volume = jnp.einsum("snom,ome->sne", combined, fields, precision=highest_value)

    west_part = jnp.einsum("nm,vme->vne", west_sel, fields, precision=highest_value)
    east_part = jnp.einsum("nm,vme->vne", east_sel, fields, precision=highest_value)
    west_beyond = jnp.concatenate([west_halo, west_part[:, :, : elements - 1]], axis=2)
    east_beyond = jnp.concatenate([east_part[:, :, 1:], east_halo], axis=2)
    lower_beyond = jnp.einsum("jn,vje->vne", take_c0, from_below, precision=highest_value)
    upper_beyond = jnp.einsum("jn,vje->vne", take_c4, from_above, precision=highest_value)
    stator_lift = jnp.einsum("vqf,fe->vqe", weight * stator, selector, precision=highest_value)
    stator_full = jnp.concatenate(
        [jnp.zeros((VARS, 100, elements), jnp.float32), stator_lift], axis=1
    )
    neighbours = west_beyond + east_beyond + lower_beyond + upper_beyond
    base_tendency = volume + weight * (neighbours - jnp.asarray(count_np) * fields) - stator_full

    top_base = fields[VARS - 1, 100:125] + segment_gain * (
        segment_decay * segment_register[VARS - 1, 100:125]
        + time_step * base_tendency[VARS - 1, 100:125]
    )
    sampled = jnp.einsum("qe,fe->qf", top_base, selector, precision=highest_value)
    surface_base = jnp.mean(sampled, axis=0)
    rotor_sum = jnp.sum(rotor_rows[VARS - 1], axis=0)

    shift = rotation[0] // face_count
    within = rotation[0] % face_count
    slots = jnp.arange(face_count, dtype=jnp.int32)
    dest_mesh = jnp.arange(mesh_size, dtype=jnp.int32)
    first = dest_mesh == (my_mesh - shift) % mesh_size
    second = dest_mesh == (my_mesh - shift - 1) % mesh_size
    keep = (first[:, None] & (slots >= within)[None, :]) | (
        second[:, None] & (slots < within)[None, :]
    )
    rotor_send = jnp.where(keep[:, None, None, :], rotor_rows[None], 0.0).reshape(mesh_size, -1)
    rotor_send = rotor_send.astype(jnp.bfloat16)
    exact = jnp.concatenate([surface_base, rotor_sum])
    exact_hi = exact.astype(jnp.bfloat16)
    exact_rest = exact - exact_hi.astype(jnp.float32)
    exact_mid = exact_rest.astype(jnp.bfloat16)
    exact_lo = (exact_rest - exact_mid.astype(jnp.float32)).astype(jnp.bfloat16)
    turn = rotation.astype(jnp.float32)
    turn_hi = turn.astype(jnp.bfloat16)
    turn_lo = (turn - turn_hi.astype(jnp.float32)).astype(jnp.bfloat16)
    shared = jnp.concatenate(
        [
            pressure_history.reshape(-1),
            surface_geometry.reshape(-1),
            face_element.astype(jnp.bfloat16),
            exact_hi,
            exact_mid,
            exact_lo,
            turn_hi,
            turn_lo,
        ]
    )
    shared_sect = lax.all_gather(shared[None], "sect", axis=0, tiled=True).reshape(-1)
    send = jnp.concatenate(
        [rotor_send, jnp.broadcast_to(shared_sect[None], (mesh_size, shared_sect.shape[0]))],
        axis=1,
    )
    recv = lax.all_to_all(send, "mesh", 0, 0, tiled=True)

    rotor_width = VARS * 25 * face_count
    near_slab = (my_mesh + shift) % mesh_size
    far_slab = (near_slab + 1) % mesh_size
    arrived = (
        lax.dynamic_index_in_dim(recv, near_slab, 0, keepdims=False)
        + lax.dynamic_index_in_dim(recv, far_slab, 0, keepdims=False)
    )[:rotor_width].astype(jnp.float32).reshape(VARS, 25, face_count)
    order = (slots + within) % face_count
    rotated = jnp.take(arrived, order, axis=2)
    rotor_lift = jnp.einsum("vqf,fe->vqe", weight * rotated, selector, precision=highest_value)
    rotor_full = jnp.concatenate(
        [jnp.zeros((VARS, 100, elements), jnp.float32), rotor_lift], axis=1
    )
    rate_tendency = base_tendency + rotor_full
    new_register = segment_decay * segment_register + time_step * rate_tendency
    new_fields = fields + segment_gain * new_register

    info = recv[:, rotor_width:].reshape(devices, shared.shape[0]).astype(jnp.float32)
    hist_rows = pressure_history.shape[0]
    geo_at = hist_rows * face_count
    fe_at = geo_at + 6 * face_count
    hi_at = fe_at + face_count
    mid_at = hi_at + 2 * face_count
    lo_at = mid_at + 2 * face_count
    turn_at = lo_at + 2 * face_count
    exact_all = (
        info[:, hi_at : hi_at + 2 * face_count] + info[:, mid_at : mid_at + 2 * face_count]
    ) + info[:, lo_at : lo_at + 2 * face_count]
    turn_all = info[:, turn_at] + info[:, turn_at + 1]
    rows = jnp.transpose(info)
    base_rows = jnp.transpose(exact_all[:, :face_count])
    all_fe = rows[fe_at : fe_at + face_count]
    all_base = base_rows
    all_sum = exact_all[:, face_count:]
    cycle = mesh_size * face_count
    by_sect = jnp.transpose(all_sum.reshape(mesh_size, sect_size, face_count), (1, 0, 2)).reshape(
        sect_size, cycle
    )
    doubled = jnp.concatenate([by_sect, by_sect], axis=1)
    rolled = jnp.stack(
        [
            lax.dynamic_slice_in_dim(doubled[k], turn_all[k].astype(jnp.int32) % cycle, cycle)
            for k in range(sect_size)
        ]
    )
    rolled = jnp.transpose(rolled.reshape(sect_size, mesh_size, face_count), (2, 1, 0)).reshape(
        face_count, devices
    )
    same = (all_fe[:, None, :] == all_fe[None, :, :]).astype(jnp.float32)
    rotor_part = jnp.sum(same * rolled[None, :, :], axis=1)
    gain = segment_gain * time_step * penalty[VARS - 1] / 25.0
    surface_now = (all_base + gain * rotor_part).astype(jnp.bfloat16)

    delays = delay_table[:, 0][None, :]
    running = jnp.zeros((TB, observer_sites.shape[1]), jnp.float32)
    for j in range(face_count):
        history = jnp.concatenate(
            [rows[j:geo_at:face_count].astype(jnp.bfloat16), surface_now[j : j + 1]], axis=0
        )
        window = jnp.zeros((TB + 1, devices), jnp.bfloat16)
        for bin_ in range(NB):
            window = jnp.where(
                delays == bin_, history[NB - 1 - bin_ : NB - 1 - bin_ + TB + 1], window
            )
        window_late = window[1:]
        change = (window_late.astype(jnp.float32) - window[:-1].astype(jnp.float32)).astype(
            jnp.bfloat16
        )
        geometry = rows[geo_at + j : fe_at : face_count]
        near_kernel, rate_kernel = far_kernels_by_observer(geometry, observer_sites)
        contract = (((1,), (1,)), ((), ()))
        running = running + lax.dot_general(
            window_late, near_kernel, contract, preferred_element_type=jnp.float32
        ) + lax.dot_general(change, rate_kernel, contract, preferred_element_type=jnp.float32)
    return (new_fields, new_register, running)


def solution(mesh):
    placed = (
        P(None, None, ALL),
        P(None, None, ALL),
        P(),
        P(),
        P(),
        P(ALL),
        P("sect"),
        P(None, ALL),
        P(None, ALL),
        P(None, ALL),
        P(None, ALL),
    )
    return jax.shard_map(
        per_device,
        mesh=mesh,
        in_specs=placed,
        out_specs=(
            P(None, None, ALL),
            P(None, None, ALL),
            P(None, ALL),
        ),
        check_vma=False,
    )
```

```python
import numpy as np
import jax
import jax.numpy as jnp
from jax import lax
from jax.sharding import PartitionSpec as P

VARS = 5
NODES = 125
FACE_DEV = 4
TB = 8
NB = 8

segment_decay = -0.4178904745
segment_gain = 1.4061
time_step = 0.2
four_pi = 12.566370614359172
highest_value = lax.Precision.HIGHEST
ALL = ("mesh", "sect")


def node_tables():
    a, b, c = np.meshgrid(np.arange(5), np.arange(5), np.arange(5), indexing="ij")
    a, b, c = a.reshape(-1), b.reshape(-1), c.reshape(-1)
    n = np.arange(NODES)
    west = np.zeros((NODES, NODES), np.float32)
    west[n[b == 0], n[b == 0] + 20] = 1.0
    east = np.zeros((NODES, NODES), np.float32)
    east[n[b == 4], n[b == 4] - 20] = 1.0
    take_c4 = np.zeros((25, NODES), np.float32)
    take_c4[np.arange(25), n[c == 4]] = 1.0
    take_c0 = np.zeros((25, NODES), np.float32)
    take_c0[np.arange(25), n[c == 0]] = 1.0
    count = ((b == 0).astype(np.float32) + (b == 4) + (c == 0) + (c == 4)).reshape(1, NODES, 1)
    return west, east, take_c4, take_c0, count


def flat_gather(value, axes):
    size = value.size
    whole = lax.all_gather(value.reshape(size), axes, axis=0, tiled=True)
    return whole.reshape((-1,) + value.shape)


def far_kernels(geometry, observers):
    separation = observers[:, None, :] - geometry[:3, :, None]
    square = jnp.sum(separation * separation, axis=0)
    radius = jnp.sqrt(square)
    normal_part = jnp.sum(geometry[3:6, :, None] * separation, axis=0)
    near_kernel = (normal_part / (four_pi * square * radius)).astype(jnp.bfloat16)
    rate_kernel = (normal_part / (four_pi * square)).astype(jnp.bfloat16)
    return (near_kernel, rate_kernel)


def far_kernels_by_observer(geometry, observers):
    separation = observers[:, :, None] - geometry[:3, None, :]
    square = jnp.sum(separation * separation, axis=0)
    radius = jnp.sqrt(square)
    normal_part = jnp.sum(geometry[3:6, None, :] * separation, axis=0)
    near_kernel = (normal_part / (four_pi * square * radius)).astype(jnp.bfloat16)
    rate_kernel = (normal_part / (four_pi * square)).astype(jnp.bfloat16)
    return (near_kernel, rate_kernel)


def per_device(
    fields,
    segment_register,
    volume_operator,
    flux_jacobian,
    penalty,
    face_element,
    rotation,
    pressure_history,
    surface_geometry,
    observer_sites,
    delay_table,
):
    elements = fields.shape[2]
    face_count = face_element.shape[0]
    west_np, east_np, take_c4_np, take_c0_np, count_np = node_tables()
    west_sel = jnp.asarray(west_np)
    east_sel = jnp.asarray(east_np)
    take_c4 = jnp.asarray(take_c4_np)
    take_c0 = jnp.asarray(take_c0_np)
    weight = penalty.reshape(VARS, 1, 1)
    mesh_size = lax.axis_size("mesh")
    sect_size = lax.axis_size("sect")
    devices = mesh_size * sect_size
    my_mesh = lax.axis_index("mesh")
    my_sect = lax.axis_index("sect")

    forward = [(i, (i + 1) % mesh_size) for i in range(mesh_size)]
    backward = [(j, i) for i, j in forward]
    west_send = jnp.einsum(
        "nm,vme->vne", west_sel, fields[:, :, elements - 1 :], precision=highest_value
    )
    east_send = jnp.einsum("nm,vme->vne", east_sel, fields[:, :, :1], precision=highest_value)
    west_halo = lax.ppermute(west_send, "mesh", forward)
    east_halo = lax.ppermute(east_send, "mesh", backward)
    upward = [(i, i + 1) for i in range(sect_size - 1)]
    downward = [(j, i) for i, j in upward]
    top_rows = fields[:, 4::5]
    bottom_rows = fields[:, 0::5]
    from_below = lax.ppermute(top_rows, "sect", upward)
    from_above = lax.ppermute(bottom_rows, "sect", downward)

    selector = (face_element[:, None] == jnp.arange(elements, dtype=jnp.int32)[None, :]).astype(
        jnp.float32
    )
    rotor_rows = jnp.einsum("vqe,fe->vqf", fields[:, 0:25], selector, precision=highest_value)
    stator = jnp.einsum("vqe,fe->vqf", fields[:, 100:125], selector, precision=highest_value)

    combined = jnp.einsum(
        "dso,dnm->snom", flux_jacobian, volume_operator, precision=highest_value
    )
    volume = jnp.einsum("snom,ome->sne", combined, fields, precision=highest_value)

    west_part = jnp.einsum("nm,vme->vne", west_sel, fields, precision=highest_value)
    east_part = jnp.einsum("nm,vme->vne", east_sel, fields, precision=highest_value)
    west_beyond = jnp.concatenate([west_halo, west_part[:, :, : elements - 1]], axis=2)
    east_beyond = jnp.concatenate([east_part[:, :, 1:], east_halo], axis=2)
    lower_beyond = jnp.einsum("jn,vje->vne", take_c0, from_below, precision=highest_value)
    upper_beyond = jnp.einsum("jn,vje->vne", take_c4, from_above, precision=highest_value)
    stator_lift = jnp.einsum("vqf,fe->vqe", weight * stator, selector, precision=highest_value)
    stator_full = jnp.concatenate(
        [jnp.zeros((VARS, 100, elements), jnp.float32), stator_lift], axis=1
    )
    neighbours = west_beyond + east_beyond + lower_beyond + upper_beyond
    base_tendency = volume + weight * (neighbours - jnp.asarray(count_np) * fields) - stator_full

    top_base = fields[VARS - 1, 100:125] + segment_gain * (
        segment_decay * segment_register[VARS - 1, 100:125]
        + time_step * base_tendency[VARS - 1, 100:125]
    )
    sampled = jnp.einsum("qe,fe->qf", top_base, selector, precision=highest_value)
    surface_base = jnp.mean(sampled, axis=0)
    rotor_sum = jnp.sum(rotor_rows[VARS - 1], axis=0)

    shift = rotation[0] // face_count
    within = rotation[0] % face_count
    slots = jnp.arange(face_count, dtype=jnp.int32)
    dest_mesh = jnp.arange(mesh_size, dtype=jnp.int32)
    first = dest_mesh == (my_mesh - shift) % mesh_size
    second = dest_mesh == (my_mesh - shift - 1) % mesh_size
    rotor_flat = rotor_rows.astype(jnp.bfloat16)
    upper_faces = jnp.where(slots >= within, rotor_flat, jnp.zeros_like(rotor_flat)).reshape(1, -1)
    lower_faces = jnp.where(slots < within, rotor_flat, jnp.zeros_like(rotor_flat)).reshape(1, -1)
    rotor_send = jnp.where(
        first[:, None],
        upper_faces,
        jnp.where(second[:, None], lower_faces, jnp.zeros_like(lower_faces)),
    )
    exact = jnp.concatenate([surface_base, rotor_sum])
    exact_hi = exact.astype(jnp.bfloat16)
    exact_rest = exact - exact_hi.astype(jnp.float32)
    exact_mid = exact_rest.astype(jnp.bfloat16)
    exact_lo = (exact_rest - exact_mid.astype(jnp.float32)).astype(jnp.bfloat16)
    turn = rotation.astype(jnp.float32)
    turn_hi = turn.astype(jnp.bfloat16)
    turn_lo = (turn - turn_hi.astype(jnp.float32)).astype(jnp.bfloat16)
    shared = jnp.concatenate(
        [
            pressure_history.reshape(-1),
            surface_geometry.reshape(-1),
            face_element.astype(jnp.bfloat16),
            exact_hi,
            exact_mid,
            exact_lo,
            turn_hi,
            turn_lo,
        ]
    )
    shared_sect = lax.all_gather(shared[None], "sect", axis=0, tiled=True).reshape(-1)
    send = jnp.concatenate(
        [rotor_send, jnp.broadcast_to(shared_sect[None], (mesh_size, shared_sect.shape[0]))],
        axis=1,
    )
    recv = lax.all_to_all(send, "mesh", 0, 0, tiled=True)

    rotor_width = VARS * 25 * face_count
    near_slab = (my_mesh + shift) % mesh_size
    far_slab = (near_slab + 1) % mesh_size
    arrived = (
        lax.dynamic_index_in_dim(recv, near_slab, 0, keepdims=False)
        + lax.dynamic_index_in_dim(recv, far_slab, 0, keepdims=False)
    )[:rotor_width].astype(jnp.float32).reshape(VARS, 25, face_count)
    order = (slots + within) % face_count
    rotated = jnp.take(arrived, order, axis=2)
    rotor_lift = jnp.einsum("vqf,fe->vqe", weight * rotated, selector, precision=highest_value)
    rotor_full = jnp.concatenate(
        [jnp.zeros((VARS, 100, elements), jnp.float32), rotor_lift], axis=1
    )
    rate_tendency = base_tendency + rotor_full
    new_register = segment_decay * segment_register + time_step * rate_tendency
    new_fields = fields + segment_gain * new_register

    info = recv[:, rotor_width:].reshape(devices, shared.shape[0]).astype(jnp.float32)
    hist_rows = pressure_history.shape[0]
    geo_at = hist_rows * face_count
    fe_at = geo_at + 6 * face_count
    hi_at = fe_at + face_count
    mid_at = hi_at + 2 * face_count
    lo_at = mid_at + 2 * face_count
    turn_at = lo_at + 2 * face_count
    exact_all = (
        info[:, hi_at : hi_at + 2 * face_count] + info[:, mid_at : mid_at + 2 * face_count]
    ) + info[:, lo_at : lo_at + 2 * face_count]
    turn_all = info[:, turn_at] + info[:, turn_at + 1]
    rows = jnp.transpose(info)
    base_rows = jnp.transpose(exact_all[:, :face_count])
    all_fe = rows[fe_at : fe_at + face_count]
    all_base = base_rows
    all_sum = exact_all[:, face_count:]
    cycle = mesh_size * face_count
    by_sect = jnp.transpose(all_sum.reshape(mesh_size, sect_size, face_count), (1, 0, 2)).reshape(
        sect_size, cycle
    )
    doubled = jnp.concatenate([by_sect, by_sect], axis=1)
    rolled = jnp.stack(
        [
            lax.dynamic_slice_in_dim(doubled[k], turn_all[k].astype(jnp.int32) % cycle, cycle)
            for k in range(sect_size)
        ]
    )
    rolled = jnp.transpose(rolled.reshape(sect_size, mesh_size, face_count), (2, 1, 0)).reshape(
        face_count, devices
    )
    same = (all_fe[:, None, :] == all_fe[None, :, :]).astype(jnp.float32)
    rotor_part = jnp.sum(same * rolled[None, :, :], axis=1)
    gain = segment_gain * time_step * penalty[VARS - 1] / 25.0
    surface_now = (all_base + gain * rotor_part).astype(jnp.bfloat16)

    delays = delay_table[:, 0][None, :]
    running = jnp.zeros((TB, observer_sites.shape[1]), jnp.float32)
    for j in range(face_count):
        history = jnp.concatenate(
            [rows[j:geo_at:face_count].astype(jnp.bfloat16), surface_now[j : j + 1]], axis=0
        )
        window = jnp.zeros((TB + 1, devices), jnp.bfloat16)
        for bin_ in range(NB):
            window = jnp.where(
                delays == bin_, history[NB - 1 - bin_ : NB - 1 - bin_ + TB + 1], window
            )
        window_late = window[1:]
        change = (window_late.astype(jnp.float32) - window[:-1].astype(jnp.float32)).astype(
            jnp.bfloat16
        )
        geometry = rows[geo_at + j : fe_at : face_count]
        near_kernel, rate_kernel = far_kernels_by_observer(geometry, observer_sites)
        contract = (((1,), (1,)), ((), ()))
        running = running + lax.dot_general(
            window_late, near_kernel, contract, preferred_element_type=jnp.float32
        ) + lax.dot_general(change, rate_kernel, contract, preferred_element_type=jnp.float32)
    return (new_fields, new_register, running)


def solution(mesh):
    placed = (
        P(None, None, ALL),
        P(None, None, ALL),
        P(),
        P(),
        P(),
        P(ALL),
        P("sect"),
        P(None, ALL),
        P(None, ALL),
        P(None, ALL),
        P(None, ALL),
    )
    return jax.shard_map(
        per_device,
        mesh=mesh,
        in_specs=placed,
        out_specs=(
            P(None, None, ALL),
            P(None, None, ALL),
            P(None, ALL),
        ),
        check_vma=False,
    )
```

```python
import numpy as np
import jax
import jax.numpy as jnp
from jax import lax
from jax.sharding import PartitionSpec as P

VARS = 5
NODES = 125
FACE_DEV = 4
TB = 8
NB = 8

segment_decay = -0.4178904745
segment_gain = 1.4061
time_step = 0.2
four_pi = 12.566370614359172
highest_value = lax.Precision.HIGHEST
ALL = ("mesh", "sect")


def node_tables():
    a, b, c = np.meshgrid(np.arange(5), np.arange(5), np.arange(5), indexing="ij")
    a, b, c = a.reshape(-1), b.reshape(-1), c.reshape(-1)
    n = np.arange(NODES)
    west = np.zeros((NODES, NODES), np.float32)
    west[n[b == 0], n[b == 0] + 20] = 1.0
    east = np.zeros((NODES, NODES), np.float32)
    east[n[b == 4], n[b == 4] - 20] = 1.0
    take_c4 = np.zeros((25, NODES), np.float32)
    take_c4[np.arange(25), n[c == 4]] = 1.0
    take_c0 = np.zeros((25, NODES), np.float32)
    take_c0[np.arange(25), n[c == 0]] = 1.0
    count = ((b == 0).astype(np.float32) + (b == 4) + (c == 0) + (c == 4)).reshape(1, NODES, 1)
    return west, east, take_c4, take_c0, count


def flat_gather(value, axes):
    size = value.size
    whole = lax.all_gather(value.reshape(size), axes, axis=0, tiled=True)
    return whole.reshape((-1,) + value.shape)


def far_kernels(geometry, observers):
    separation = observers[:, None, :] - geometry[:3, :, None]
    square = jnp.sum(separation * separation, axis=0)
    radius = jnp.sqrt(square)
    normal_part = jnp.sum(geometry[3:6, :, None] * separation, axis=0)
    near_kernel = (normal_part / (four_pi * square * radius)).astype(jnp.bfloat16)
    rate_kernel = (normal_part / (four_pi * square)).astype(jnp.bfloat16)
    return (near_kernel, rate_kernel)


def far_kernels_by_observer(geometry, observers):
    separation = observers[:, :, None] - geometry[:3, None, :]
    square = jnp.sum(separation * separation, axis=0)
    radius = jnp.sqrt(square)
    normal_part = jnp.sum(geometry[3:6, None, :] * separation, axis=0)
    near_kernel = (normal_part / (four_pi * square * radius)).astype(jnp.bfloat16)
    rate_kernel = (normal_part / (four_pi * square)).astype(jnp.bfloat16)
    return (near_kernel, rate_kernel)


def per_device(
    fields,
    segment_register,
    volume_operator,
    flux_jacobian,
    penalty,
    face_element,
    rotation,
    pressure_history,
    surface_geometry,
    observer_sites,
    delay_table,
):
    elements = fields.shape[2]
    face_count = face_element.shape[0]
    west_np, east_np, take_c4_np, take_c0_np, count_np = node_tables()
    west_sel = jnp.asarray(west_np)
    east_sel = jnp.asarray(east_np)
    take_c4 = jnp.asarray(take_c4_np)
    take_c0 = jnp.asarray(take_c0_np)
    weight = penalty.reshape(VARS, 1, 1)
    mesh_size = lax.axis_size("mesh")
    sect_size = lax.axis_size("sect")
    devices = mesh_size * sect_size
    my_mesh = lax.axis_index("mesh")
    my_sect = lax.axis_index("sect")

    forward = [(i, (i + 1) % mesh_size) for i in range(mesh_size)]
    backward = [(j, i) for i, j in forward]
    west_send = jnp.einsum(
        "nm,vme->vne", west_sel, fields[:, :, elements - 1 :], precision=highest_value
    )
    east_send = jnp.einsum("nm,vme->vne", east_sel, fields[:, :, :1], precision=highest_value)
    west_halo = lax.ppermute(west_send, "mesh", forward)
    east_halo = lax.ppermute(east_send, "mesh", backward)
    upward = [(i, i + 1) for i in range(sect_size - 1)]
    downward = [(j, i) for i, j in upward]
    top_rows = fields[:, 4::5]
    bottom_rows = fields[:, 0::5]
    from_below = lax.ppermute(top_rows, "sect", upward)
    from_above = lax.ppermute(bottom_rows, "sect", downward)

    selector = (face_element[:, None] == jnp.arange(elements, dtype=jnp.int32)[None, :]).astype(
        jnp.float32
    )
    rotor_rows = jnp.einsum("vqe,fe->vqf", fields[:, 0:25], selector, precision=highest_value)
    stator = jnp.einsum("vqe,fe->vqf", fields[:, 100:125], selector, precision=highest_value)

    combined = jnp.einsum(
        "dso,dnm->snom", flux_jacobian, volume_operator, precision=highest_value
    )
    volume = jnp.einsum("snom,ome->sne", combined, fields, precision=highest_value)

    west_part = jnp.einsum("nm,vme->vne", west_sel, fields, precision=highest_value)
    east_part = jnp.einsum("nm,vme->vne", east_sel, fields, precision=highest_value)
    west_beyond = jnp.concatenate([west_halo, west_part[:, :, : elements - 1]], axis=2)
    east_beyond = jnp.concatenate([east_part[:, :, 1:], east_halo], axis=2)
    lower_beyond = jnp.einsum("jn,vje->vne", take_c0, from_below, precision=highest_value)
    upper_beyond = jnp.einsum("jn,vje->vne", take_c4, from_above, precision=highest_value)
    stator_lift = jnp.einsum("vqf,fe->vqe", weight * stator, selector, precision=highest_value)
    stator_full = jnp.concatenate(
        [jnp.zeros((VARS, 100, elements), jnp.float32), stator_lift], axis=1
    )
    neighbours = west_beyond + east_beyond + lower_beyond + upper_beyond
    base_tendency = volume + weight * (neighbours - jnp.asarray(count_np) * fields) - stator_full

    top_base = fields[VARS - 1, 100:125] + segment_gain * (
        segment_decay * segment_register[VARS - 1, 100:125]
        + time_step * base_tendency[VARS - 1, 100:125]
    )
    sampled = jnp.einsum("qe,fe->qf", top_base, selector, precision=highest_value)
    surface_base = jnp.mean(sampled, axis=0)
    rotor_sum = jnp.sum(rotor_rows[VARS - 1], axis=0)

    shift = rotation[0] // face_count
    within = rotation[0] % face_count
    slots = jnp.arange(face_count, dtype=jnp.int32)
    dest_mesh = jnp.arange(mesh_size, dtype=jnp.int32)
    first = dest_mesh == (my_mesh - shift) % mesh_size
    second = dest_mesh == (my_mesh - shift - 1) % mesh_size
    rotor_flat = rotor_rows.astype(jnp.bfloat16)
    upper_faces = jnp.where(slots >= within, rotor_flat, jnp.zeros_like(rotor_flat)).reshape(1, -1)
    lower_faces = jnp.where(slots < within, rotor_flat, jnp.zeros_like(rotor_flat)).reshape(1, -1)
    rotor_send = jnp.where(
        first[:, None],
        upper_faces,
        jnp.where(second[:, None], lower_faces, jnp.zeros_like(lower_faces)),
    )
    exact = jnp.concatenate([surface_base, rotor_sum])
    exact_hi = exact.astype(jnp.bfloat16)
    exact_rest = exact - exact_hi.astype(jnp.float32)
    exact_mid = exact_rest.astype(jnp.bfloat16)
    exact_lo = (exact_rest - exact_mid.astype(jnp.float32)).astype(jnp.bfloat16)
    turn = rotation.astype(jnp.float32)
    turn_hi = turn.astype(jnp.bfloat16)
    turn_lo = (turn - turn_hi.astype(jnp.float32)).astype(jnp.bfloat16)
    shared = jnp.concatenate(
        [
            pressure_history.reshape(-1),
            surface_geometry.reshape(-1),
            face_element.astype(jnp.bfloat16),
            exact_hi,
            exact_mid,
            exact_lo,
            turn_hi,
            turn_lo,
        ]
    )
    shared_sect = lax.all_gather(shared[None], "sect", axis=0, tiled=True).reshape(-1)
    send = jnp.concatenate(
        [rotor_send, jnp.broadcast_to(shared_sect[None], (mesh_size, shared_sect.shape[0]))],
        axis=1,
    )
    recv = lax.all_to_all(send, "mesh", 0, 0, tiled=True)

    rotor_width = VARS * 25 * face_count
    near_slab = (my_mesh + shift) % mesh_size
    far_slab = (near_slab + 1) % mesh_size
    arrived = (
        lax.dynamic_index_in_dim(recv, near_slab, 0, keepdims=False)
        + lax.dynamic_index_in_dim(recv, far_slab, 0, keepdims=False)
    )[:rotor_width].astype(jnp.float32).reshape(VARS, 25, face_count)
    order = (slots + within) % face_count
    rotated = jnp.take(arrived, order, axis=2)
    rotor_lift = jnp.einsum("vqf,fe->vqe", weight * rotated, selector, precision=highest_value)
    rotor_full = jnp.concatenate(
        [jnp.zeros((VARS, 100, elements), jnp.float32), rotor_lift], axis=1
    )
    rate_tendency = base_tendency + rotor_full
    new_register = segment_decay * segment_register + time_step * rate_tendency
    new_fields = fields + segment_gain * new_register

    info = recv[:, rotor_width:].reshape(devices, shared.shape[0]).astype(jnp.float32)
    hist_rows = pressure_history.shape[0]
    geo_at = hist_rows * face_count
    fe_at = geo_at + 6 * face_count
    hi_at = fe_at + face_count
    mid_at = hi_at + 2 * face_count
    lo_at = mid_at + 2 * face_count
    turn_at = lo_at + 2 * face_count
    exact_all = (
        info[:, hi_at : hi_at + 2 * face_count] + info[:, mid_at : mid_at + 2 * face_count]
    ) + info[:, lo_at : lo_at + 2 * face_count]
    turn_all = info[:, turn_at] + info[:, turn_at + 1]
    rows = jnp.transpose(info)
    base_rows = jnp.transpose(exact_all[:, :face_count])
    all_fe = rows[fe_at : fe_at + face_count]
    all_base = base_rows
    all_sum = exact_all[:, face_count:]
    cycle = mesh_size * face_count
    by_sect = jnp.transpose(all_sum.reshape(mesh_size, sect_size, face_count), (1, 0, 2)).reshape(
        sect_size, cycle
    )
    doubled = jnp.concatenate([by_sect, by_sect], axis=1)
    rolled = jnp.stack(
        [
            lax.dynamic_slice_in_dim(doubled[k], turn_all[k].astype(jnp.int32) % cycle, cycle)
            for k in range(sect_size)
        ]
    )
    rolled = jnp.transpose(rolled.reshape(sect_size, mesh_size, face_count), (2, 1, 0)).reshape(
        face_count, devices
    )
    same = (all_fe[:, None, :] == all_fe[None, :, :]).astype(jnp.float32)
    rotor_part = jnp.sum(same * rolled[None, :, :], axis=1)
    gain = segment_gain * time_step * penalty[VARS - 1] / 25.0
    surface_now = (all_base + gain * rotor_part).astype(jnp.bfloat16)

    delays = delay_table[:, 0][None, :]
    old_rows = rows[0:geo_at].reshape(hist_rows, face_count, devices)
    history = jnp.concatenate(
        [jnp.transpose(old_rows, (1, 0, 2)).astype(jnp.bfloat16), surface_now[:, None, :]],
        axis=1,
    )
    window = jnp.zeros((face_count, TB + 1, devices), jnp.bfloat16)
    for bin_ in range(NB):
        window = jnp.where(
            (delays == bin_)[None], history[:, NB - 1 - bin_ : NB - 1 - bin_ + TB + 1], window
        )
    window_late = window[:, 1:]
    change = (window_late.astype(jnp.float32) - window[:, :-1].astype(jnp.float32)).astype(
        jnp.bfloat16
    )
    geometry = rows[geo_at:fe_at].reshape(6, face_count, devices)
    separation = observer_sites[:, None, :, None] - geometry[:3, :, None, :]
    square = jnp.sum(separation * separation, axis=0)
    radius = jnp.sqrt(square)
    normal_part = jnp.sum(geometry[3:6, :, None, :] * separation, axis=0)
    near_kernel = (normal_part / (four_pi * square * radius)).astype(jnp.bfloat16)
    rate_kernel = (normal_part / (four_pi * square)).astype(jnp.bfloat16)
    contract = (((0, 2), (0, 2)), ((), ()))
    running = lax.dot_general(
        window_late, near_kernel, contract, preferred_element_type=jnp.float32
    ) + lax.dot_general(change, rate_kernel, contract, preferred_element_type=jnp.float32)
    return (new_fields, new_register, running)


def solution(mesh):
    placed = (
        P(None, None, ALL),
        P(None, None, ALL),
        P(),
        P(),
        P(),
        P(ALL),
        P("sect"),
        P(None, ALL),
        P(None, ALL),
        P(None, ALL),
        P(None, ALL),
    )
    return jax.shard_map(
        per_device,
        mesh=mesh,
        in_specs=placed,
        out_specs=(
            P(None, None, ALL),
            P(None, None, ALL),
            P(None, ALL),
        ),
        check_vma=False,
    )
```

```python
import numpy as np
import jax
import jax.numpy as jnp
from jax import lax
from jax.sharding import PartitionSpec as P

VARS = 5
NODES = 125
FACE_DEV = 4
TB = 8
NB = 8

segment_decay = -0.4178904745
segment_gain = 1.4061
time_step = 0.2
four_pi = 12.566370614359172
highest_value = lax.Precision.HIGHEST
ALL = ("mesh", "sect")


def node_tables():
    a, b, c = np.meshgrid(np.arange(5), np.arange(5), np.arange(5), indexing="ij")
    a, b, c = a.reshape(-1), b.reshape(-1), c.reshape(-1)
    n = np.arange(NODES)
    west = np.zeros((NODES, NODES), np.float32)
    west[n[b == 0], n[b == 0] + 20] = 1.0
    east = np.zeros((NODES, NODES), np.float32)
    east[n[b == 4], n[b == 4] - 20] = 1.0
    take_c4 = np.zeros((25, NODES), np.float32)
    take_c4[np.arange(25), n[c == 4]] = 1.0
    take_c0 = np.zeros((25, NODES), np.float32)
    take_c0[np.arange(25), n[c == 0]] = 1.0
    count = ((b == 0).astype(np.float32) + (b == 4) + (c == 0) + (c == 4)).reshape(1, NODES, 1)
    return west, east, take_c4, take_c0, count


def flat_gather(value, axes):
    size = value.size
    whole = lax.all_gather(value.reshape(size), axes, axis=0, tiled=True)
    return whole.reshape((-1,) + value.shape)


def far_kernels(geometry, observers):
    separation = observers[:, None, :] - geometry[:3, :, None]
    square = jnp.sum(separation * separation, axis=0)
    radius = jnp.sqrt(square)
    normal_part = jnp.sum(geometry[3:6, :, None] * separation, axis=0)
    near_kernel = (normal_part / (four_pi * square * radius)).astype(jnp.bfloat16)
    rate_kernel = (normal_part / (four_pi * square)).astype(jnp.bfloat16)
    return (near_kernel, rate_kernel)


def far_kernels_by_observer(geometry, observers):
    separation = observers[:, :, None] - geometry[:3, None, :]
    square = jnp.sum(separation * separation, axis=0)
    radius = jnp.sqrt(square)
    normal_part = jnp.sum(geometry[3:6, None, :] * separation, axis=0)
    near_kernel = (normal_part / (four_pi * square * radius)).astype(jnp.bfloat16)
    rate_kernel = (normal_part / (four_pi * square)).astype(jnp.bfloat16)
    return (near_kernel, rate_kernel)


def per_device(
    fields,
    segment_register,
    volume_operator,
    flux_jacobian,
    penalty,
    face_element,
    rotation,
    pressure_history,
    surface_geometry,
    observer_sites,
    delay_table,
):
    elements = fields.shape[2]
    face_count = face_element.shape[0]
    west_np, east_np, take_c4_np, take_c0_np, count_np = node_tables()
    west_sel = jnp.asarray(west_np)
    east_sel = jnp.asarray(east_np)
    take_c4 = jnp.asarray(take_c4_np)
    take_c0 = jnp.asarray(take_c0_np)
    weight = penalty.reshape(VARS, 1, 1)
    mesh_size = lax.axis_size("mesh")
    sect_size = lax.axis_size("sect")
    devices = mesh_size * sect_size
    my_mesh = lax.axis_index("mesh")
    my_sect = lax.axis_index("sect")

    forward = [(i, (i + 1) % mesh_size) for i in range(mesh_size)]
    backward = [(j, i) for i, j in forward]
    west_raw = lax.ppermute(fields[:, :, elements - 1 :], "mesh", forward)
    east_raw = lax.ppermute(fields[:, :, :1], "mesh", backward)
    west_halo = jnp.einsum("nm,vme->vne", west_sel, west_raw, precision=highest_value)
    east_halo = jnp.einsum("nm,vme->vne", east_sel, east_raw, precision=highest_value)
    upward = [(i, i + 1) for i in range(sect_size - 1)]
    downward = [(j, i) for i, j in upward]
    top_rows = fields[:, 4::5]
    bottom_rows = fields[:, 0::5]
    from_below = lax.ppermute(top_rows, "sect", upward)
    from_above = lax.ppermute(bottom_rows, "sect", downward)

    selector = (face_element[:, None] == jnp.arange(elements, dtype=jnp.int32)[None, :]).astype(
        jnp.float32
    )
    rotor_rows = jnp.einsum("vqe,fe->vqf", fields[:, 0:25], selector, precision=highest_value)
    stator = jnp.einsum("vqe,fe->vqf", fields[:, 100:125], selector, precision=highest_value)

    combined = jnp.einsum(
        "dso,dnm->snom", flux_jacobian, volume_operator, precision=highest_value
    )
    volume = jnp.einsum("snom,ome->sne", combined, fields, precision=highest_value)

    west_part = jnp.einsum("nm,vme->vne", west_sel, fields, precision=highest_value)
    east_part = jnp.einsum("nm,vme->vne", east_sel, fields, precision=highest_value)
    west_beyond = jnp.concatenate([west_halo, west_part[:, :, : elements - 1]], axis=2)
    east_beyond = jnp.concatenate([east_part[:, :, 1:], east_halo], axis=2)
    lower_beyond = jnp.einsum("jn,vje->vne", take_c0, from_below, precision=highest_value)
    upper_beyond = jnp.einsum("jn,vje->vne", take_c4, from_above, precision=highest_value)
    stator_lift = jnp.einsum("vqf,fe->vqe", weight * stator, selector, precision=highest_value)
    stator_full = jnp.concatenate(
        [jnp.zeros((VARS, 100, elements), jnp.float32), stator_lift], axis=1
    )
    neighbours = west_beyond + east_beyond + lower_beyond + upper_beyond
    base_tendency = volume + weight * (neighbours - jnp.asarray(count_np) * fields) - stator_full

    top_base = fields[VARS - 1, 100:125] + segment_gain * (
        segment_decay * segment_register[VARS - 1, 100:125]
        + time_step * base_tendency[VARS - 1, 100:125]
    )
    sampled = jnp.einsum("qe,fe->qf", top_base, selector, precision=highest_value)
    surface_base = jnp.mean(sampled, axis=0)
    rotor_sum = jnp.sum(rotor_rows[VARS - 1], axis=0)

    shift = rotation[0] // face_count
    within = rotation[0] % face_count
    slots = jnp.arange(face_count, dtype=jnp.int32)
    dest_mesh = jnp.arange(mesh_size, dtype=jnp.int32)
    first = dest_mesh == (my_mesh - shift) % mesh_size
    second = dest_mesh == (my_mesh - shift - 1) % mesh_size
    keep = (first[:, None] & (slots >= within)[None, :]) | (
        second[:, None] & (slots < within)[None, :]
    )
    rotor_send = jnp.where(keep[:, None, None, :], rotor_rows[None], 0.0).reshape(mesh_size, -1)
    rotor_send = rotor_send.astype(jnp.bfloat16)
    exact = jnp.concatenate([surface_base, rotor_sum])
    exact_hi = exact.astype(jnp.bfloat16)
    exact_rest = exact - exact_hi.astype(jnp.float32)
    exact_mid = exact_rest.astype(jnp.bfloat16)
    exact_lo = (exact_rest - exact_mid.astype(jnp.float32)).astype(jnp.bfloat16)
    turn = rotation.astype(jnp.float32)
    turn_hi = turn.astype(jnp.bfloat16)
    turn_lo = (turn - turn_hi.astype(jnp.float32)).astype(jnp.bfloat16)
    shared = jnp.concatenate(
        [
            pressure_history.reshape(-1),
            surface_geometry.reshape(-1),
            face_element.astype(jnp.bfloat16),
            exact_hi,
            exact_mid,
            exact_lo,
            turn_hi,
            turn_lo,
        ]
    )
    shared_sect = lax.all_gather(shared[None], "sect", axis=0, tiled=True).reshape(-1)
    send = jnp.concatenate(
        [rotor_send, jnp.broadcast_to(shared_sect[None], (mesh_size, shared_sect.shape[0]))],
        axis=1,
    )
    recv = lax.all_to_all(send, "mesh", 0, 0, tiled=True)

    rotor_width = VARS * 25 * face_count
    near_slab = (my_mesh + shift) % mesh_size
    far_slab = (near_slab + 1) % mesh_size
    arrived = (
        lax.dynamic_index_in_dim(recv, near_slab, 0, keepdims=False)
        + lax.dynamic_index_in_dim(recv, far_slab, 0, keepdims=False)
    )[:rotor_width].astype(jnp.float32).reshape(VARS, 25, face_count)
    order = (slots + within) % face_count
    rotated = jnp.take(arrived, order, axis=2)
    rotor_lift = jnp.einsum("vqf,fe->vqe", weight * rotated, selector, precision=highest_value)
    rotor_full = jnp.concatenate(
        [jnp.zeros((VARS, 100, elements), jnp.float32), rotor_lift], axis=1
    )
    rate_tendency = base_tendency + rotor_full
    new_register = segment_decay * segment_register + time_step * rate_tendency
    new_fields = fields + segment_gain * new_register

    info = recv[:, rotor_width:].reshape(devices, shared.shape[0]).astype(jnp.float32)
    hist_rows = pressure_history.shape[0]
    geo_at = hist_rows * face_count
    fe_at = geo_at + 6 * face_count
    hi_at = fe_at + face_count
    mid_at = hi_at + 2 * face_count
    lo_at = mid_at + 2 * face_count
    turn_at = lo_at + 2 * face_count
    exact_all = (
        info[:, hi_at : hi_at + 2 * face_count] + info[:, mid_at : mid_at + 2 * face_count]
    ) + info[:, lo_at : lo_at + 2 * face_count]
    turn_all = info[:, turn_at] + info[:, turn_at + 1]
    rows = jnp.transpose(info)
    base_rows = jnp.transpose(exact_all[:, :face_count])
    all_fe = rows[fe_at : fe_at + face_count]
    all_base = base_rows
    all_sum = exact_all[:, face_count:]
    cycle = mesh_size * face_count
    by_sect = jnp.transpose(all_sum.reshape(mesh_size, sect_size, face_count), (1, 0, 2)).reshape(
        sect_size, cycle
    )
    doubled = jnp.concatenate([by_sect, by_sect], axis=1)
    rolled = jnp.stack(
        [
            lax.dynamic_slice_in_dim(doubled[k], turn_all[k].astype(jnp.int32) % cycle, cycle)
            for k in range(sect_size)
        ]
    )
    rolled = jnp.transpose(rolled.reshape(sect_size, mesh_size, face_count), (2, 1, 0)).reshape(
        face_count, devices
    )
    same = (all_fe[:, None, :] == all_fe[None, :, :]).astype(jnp.float32)
    rotor_part = jnp.sum(same * rolled[None, :, :], axis=1)
    gain = segment_gain * time_step * penalty[VARS - 1] / 25.0
    surface_now = (all_base + gain * rotor_part).astype(jnp.bfloat16)

    delays = delay_table[:, 0][None, :]
    running = jnp.zeros((TB, observer_sites.shape[1]), jnp.float32)
    for j in range(face_count):
        history = jnp.concatenate(
            [rows[j:geo_at:face_count].astype(jnp.bfloat16), surface_now[j : j + 1]], axis=0
        )
        window = jnp.zeros((TB + 1, devices), jnp.bfloat16)
        for bin_ in range(NB):
            window = jnp.where(
                delays == bin_, history[NB - 1 - bin_ : NB - 1 - bin_ + TB + 1], window
            )
        window_late = window[1:]
        change = (window_late.astype(jnp.float32) - window[:-1].astype(jnp.float32)).astype(
            jnp.bfloat16
        )
        geometry = rows[geo_at + j : fe_at : face_count]
        near_kernel, rate_kernel = far_kernels_by_observer(geometry, observer_sites)
        contract = (((1,), (1,)), ((), ()))
        running = running + lax.dot_general(
            window_late, near_kernel, contract, preferred_element_type=jnp.float32
        ) + lax.dot_general(change, rate_kernel, contract, preferred_element_type=jnp.float32)
    return (new_fields, new_register, running)


def solution(mesh):
    placed = (
        P(None, None, ALL),
        P(None, None, ALL),
        P(),
        P(),
        P(),
        P(ALL),
        P("sect"),
        P(None, ALL),
        P(None, ALL),
        P(None, ALL),
        P(None, ALL),
    )
    return jax.shard_map(
        per_device,
        mesh=mesh,
        in_specs=placed,
        out_specs=(
            P(None, None, ALL),
            P(None, None, ALL),
            P(None, ALL),
        ),
        check_vma=False,
    )
```

```python
import numpy as np
import jax
import jax.numpy as jnp
from jax import lax
from jax.sharding import PartitionSpec as P

VARS = 5
NODES = 125
FACE_DEV = 4
TB = 8
NB = 8

segment_decay = -0.4178904745
segment_gain = 1.4061
time_step = 0.2
four_pi = 12.566370614359172
highest_value = lax.Precision.HIGHEST
ALL = ("mesh", "sect")


def node_tables():
    a, b, c = np.meshgrid(np.arange(5), np.arange(5), np.arange(5), indexing="ij")
    a, b, c = a.reshape(-1), b.reshape(-1), c.reshape(-1)
    n = np.arange(NODES)
    west = np.zeros((NODES, NODES), np.float32)
    west[n[b == 0], n[b == 0] + 20] = 1.0
    east = np.zeros((NODES, NODES), np.float32)
    east[n[b == 4], n[b == 4] - 20] = 1.0
    take_c4 = np.zeros((25, NODES), np.float32)
    take_c4[np.arange(25), n[c == 4]] = 1.0
    take_c0 = np.zeros((25, NODES), np.float32)
    take_c0[np.arange(25), n[c == 0]] = 1.0
    count = ((b == 0).astype(np.float32) + (b == 4) + (c == 0) + (c == 4)).reshape(1, NODES, 1)
    return west, east, take_c4, take_c0, count


def flat_gather(value, axes):
    size = value.size
    whole = lax.all_gather(value.reshape(size), axes, axis=0, tiled=True)
    return whole.reshape((-1,) + value.shape)


def far_kernels(geometry, observers):
    separation = observers[:, None, :] - geometry[:3, :, None]
    square = jnp.sum(separation * separation, axis=0)
    radius = jnp.sqrt(square)
    normal_part = jnp.sum(geometry[3:6, :, None] * separation, axis=0)
    near_kernel = (normal_part / (four_pi * square * radius)).astype(jnp.bfloat16)
    rate_kernel = (normal_part / (four_pi * square)).astype(jnp.bfloat16)
    return (near_kernel, rate_kernel)


def far_kernels_by_observer(geometry, observers):
    separation = observers[:, :, None] - geometry[:3, None, :]
    square = jnp.sum(separation * separation, axis=0)
    radius = jnp.sqrt(square)
    normal_part = jnp.sum(geometry[3:6, None, :] * separation, axis=0)
    near_kernel = (normal_part / (four_pi * square * radius)).astype(jnp.bfloat16)
    rate_kernel = (normal_part / (four_pi * square)).astype(jnp.bfloat16)
    return (near_kernel, rate_kernel)


def per_device(
    fields,
    segment_register,
    volume_operator,
    flux_jacobian,
    penalty,
    face_element,
    rotation,
    pressure_history,
    surface_geometry,
    observer_sites,
    delay_table,
):
    elements = fields.shape[2]
    face_count = face_element.shape[0]
    west_np, east_np, take_c4_np, take_c0_np, count_np = node_tables()
    west_sel = jnp.asarray(west_np)
    east_sel = jnp.asarray(east_np)
    take_c4 = jnp.asarray(take_c4_np)
    take_c0 = jnp.asarray(take_c0_np)
    weight = penalty.reshape(VARS, 1, 1)
    mesh_size = lax.axis_size("mesh")
    sect_size = lax.axis_size("sect")
    devices = mesh_size * sect_size
    my_mesh = lax.axis_index("mesh")
    my_sect = lax.axis_index("sect")

    forward = [(i, (i + 1) % mesh_size) for i in range(mesh_size)]
    backward = [(j, i) for i, j in forward]
    west_raw = lax.ppermute(fields[:, :, elements - 1 :], "mesh", forward)
    east_raw = lax.ppermute(fields[:, :, :1], "mesh", backward)
    west_halo = jnp.einsum("nm,vme->vne", west_sel, west_raw, precision=highest_value)
    east_halo = jnp.einsum("nm,vme->vne", east_sel, east_raw, precision=highest_value)
    upward = [(i, i + 1) for i in range(sect_size - 1)]
    downward = [(j, i) for i, j in upward]
    top_rows = fields[:, 4::5]
    bottom_rows = fields[:, 0::5]
    from_below = lax.ppermute(top_rows, "sect", upward)
    from_above = lax.ppermute(bottom_rows, "sect", downward)

    selector = (face_element[:, None] == jnp.arange(elements, dtype=jnp.int32)[None, :]).astype(
        jnp.float32
    )
    rotor_rows = jnp.einsum("vqe,fe->vqf", fields[:, 0:25], selector, precision=highest_value)
    stator = jnp.einsum("vqe,fe->vqf", fields[:, 100:125], selector, precision=highest_value)

    combined = jnp.einsum(
        "dso,dnm->snom", flux_jacobian, volume_operator, precision=highest_value
    )
    volume = jnp.einsum("snom,ome->sne", combined, fields, precision=highest_value)

    west_part = jnp.einsum("nm,vme->vne", west_sel, fields, precision=highest_value)
    east_part = jnp.einsum("nm,vme->vne", east_sel, fields, precision=highest_value)
    west_beyond = jnp.concatenate([west_halo, west_part[:, :, : elements - 1]], axis=2)
    east_beyond = jnp.concatenate([east_part[:, :, 1:], east_halo], axis=2)
    lower_beyond = jnp.einsum("jn,vje->vne", take_c0, from_below, precision=highest_value)
    upper_beyond = jnp.einsum("jn,vje->vne", take_c4, from_above, precision=highest_value)
    stator_lift = jnp.einsum("vqf,fe->vqe", weight * stator, selector, precision=highest_value)
    stator_full = jnp.concatenate(
        [jnp.zeros((VARS, 100, elements), jnp.float32), stator_lift], axis=1
    )
    neighbours = west_beyond + east_beyond + lower_beyond + upper_beyond
    base_tendency = volume + weight * (neighbours - jnp.asarray(count_np) * fields) - stator_full

    top_base = fields[VARS - 1, 100:125] + segment_gain * (
        segment_decay * segment_register[VARS - 1, 100:125]
        + time_step * base_tendency[VARS - 1, 100:125]
    )
    sampled = jnp.einsum("qe,fe->qf", top_base, selector, precision=highest_value)
    surface_base = jnp.mean(sampled, axis=0)
    rotor_sum = jnp.sum(rotor_rows[VARS - 1], axis=0)

    shift = rotation[0] // face_count
    within = rotation[0] % face_count
    slots = jnp.arange(face_count, dtype=jnp.int32)
    dest_mesh = jnp.arange(mesh_size, dtype=jnp.int32)
    first = dest_mesh == (my_mesh - shift) % mesh_size
    second = dest_mesh == (my_mesh - shift - 1) % mesh_size
    rotor_flat = rotor_rows.astype(jnp.bfloat16)
    upper_faces = jnp.where(slots >= within, rotor_flat, jnp.zeros_like(rotor_flat)).reshape(1, -1)
    lower_faces = jnp.where(slots < within, rotor_flat, jnp.zeros_like(rotor_flat)).reshape(1, -1)
    rotor_send = jnp.where(
        first[:, None],
        upper_faces,
        jnp.where(second[:, None], lower_faces, jnp.zeros_like(lower_faces)),
    )
    exact = jnp.concatenate([surface_base, rotor_sum])
    exact_hi = exact.astype(jnp.bfloat16)
    exact_rest = exact - exact_hi.astype(jnp.float32)
    exact_mid = exact_rest.astype(jnp.bfloat16)
    exact_lo = (exact_rest - exact_mid.astype(jnp.float32)).astype(jnp.bfloat16)
    turn = rotation.astype(jnp.float32)
    turn_hi = turn.astype(jnp.bfloat16)
    turn_lo = (turn - turn_hi.astype(jnp.float32)).astype(jnp.bfloat16)
    shared = jnp.concatenate(
        [
            pressure_history.reshape(-1),
            surface_geometry.reshape(-1),
            face_element.astype(jnp.bfloat16),
            exact_hi,
            exact_mid,
            exact_lo,
            turn_hi,
            turn_lo,
        ]
    )
    shared_sect = lax.all_gather(shared[None], "sect", axis=0, tiled=True).reshape(-1)
    send = jnp.concatenate(
        [rotor_send, jnp.broadcast_to(shared_sect[None], (mesh_size, shared_sect.shape[0]))],
        axis=1,
    )
    recv = lax.all_to_all(send, "mesh", 0, 0, tiled=True)

    rotor_width = VARS * 25 * face_count
    near_slab = (my_mesh + shift) % mesh_size
    far_slab = (near_slab + 1) % mesh_size
    arrived = (
        lax.dynamic_index_in_dim(recv, near_slab, 0, keepdims=False)
        + lax.dynamic_index_in_dim(recv, far_slab, 0, keepdims=False)
    )[:rotor_width].astype(jnp.float32).reshape(VARS, 25, face_count)
    order = (slots + within) % face_count
    rotated = jnp.take(arrived, order, axis=2)
    rotor_lift = jnp.einsum("vqf,fe->vqe", weight * rotated, selector, precision=highest_value)
    rotor_full = jnp.concatenate(
        [jnp.zeros((VARS, 100, elements), jnp.float32), rotor_lift], axis=1
    )
    rate_tendency = base_tendency + rotor_full
    new_register = segment_decay * segment_register + time_step * rate_tendency
    new_fields = fields + segment_gain * new_register

    info = recv[:, rotor_width:].reshape(devices, shared.shape[0]).astype(jnp.float32)
    hist_rows = pressure_history.shape[0]
    geo_at = hist_rows * face_count
    fe_at = geo_at + 6 * face_count
    hi_at = fe_at + face_count
    mid_at = hi_at + 2 * face_count
    lo_at = mid_at + 2 * face_count
    turn_at = lo_at + 2 * face_count
    exact_all = (
        info[:, hi_at : hi_at + 2 * face_count] + info[:, mid_at : mid_at + 2 * face_count]
    ) + info[:, lo_at : lo_at + 2 * face_count]
    turn_all = info[:, turn_at] + info[:, turn_at + 1]
    rows = jnp.transpose(info)
    base_rows = jnp.transpose(exact_all[:, :face_count])
    all_fe = rows[fe_at : fe_at + face_count]
    all_base = base_rows
    all_sum = exact_all[:, face_count:]
    cycle = mesh_size * face_count
    by_sect = jnp.transpose(all_sum.reshape(mesh_size, sect_size, face_count), (1, 0, 2)).reshape(
        sect_size, cycle
    )
    doubled = jnp.concatenate([by_sect, by_sect], axis=1)
    rolled = jnp.stack(
        [
            lax.dynamic_slice_in_dim(doubled[k], turn_all[k].astype(jnp.int32) % cycle, cycle)
            for k in range(sect_size)
        ]
    )
    rolled = jnp.transpose(rolled.reshape(sect_size, mesh_size, face_count), (2, 1, 0)).reshape(
        face_count, devices
    )
    same = (all_fe[:, None, :] == all_fe[None, :, :]).astype(jnp.float32)
    rotor_part = jnp.sum(same * rolled[None, :, :], axis=1)
    gain = segment_gain * time_step * penalty[VARS - 1] / 25.0
    surface_now = (all_base + gain * rotor_part).astype(jnp.bfloat16)

    delays = delay_table[:, 0][None, :]
    running = jnp.zeros((TB, observer_sites.shape[1]), jnp.float32)
    for j in range(face_count):
        history = jnp.concatenate(
            [rows[j:geo_at:face_count].astype(jnp.bfloat16), surface_now[j : j + 1]], axis=0
        )
        window = jnp.zeros((TB + 1, devices), jnp.bfloat16)
        for bin_ in range(NB):
            window = jnp.where(
                delays == bin_, history[NB - 1 - bin_ : NB - 1 - bin_ + TB + 1], window
            )
        window_late = window[1:]
        change = (window_late.astype(jnp.float32) - window[:-1].astype(jnp.float32)).astype(
            jnp.bfloat16
        )
        geometry = rows[geo_at + j : fe_at : face_count]
        near_kernel, rate_kernel = far_kernels_by_observer(geometry, observer_sites)
        contract = (((1,), (1,)), ((), ()))
        running = running + lax.dot_general(
            window_late, near_kernel, contract, preferred_element_type=jnp.float32
        ) + lax.dot_general(change, rate_kernel, contract, preferred_element_type=jnp.float32)
    return (new_fields, new_register, running)


def solution(mesh):
    placed = (
        P(None, None, ALL),
        P(None, None, ALL),
        P(),
        P(),
        P(),
        P(ALL),
        P("sect"),
        P(None, ALL),
        P(None, ALL),
        P(None, ALL),
        P(None, ALL),
    )
    return jax.shard_map(
        per_device,
        mesh=mesh,
        in_specs=placed,
        out_specs=(
            P(None, None, ALL),
            P(None, None, ALL),
            P(None, ALL),
        ),
        check_vma=False,
    )
```
